512 devices in a mesh: seg: 16 (over z, x_lo), tok: 32 (over x_hi, y, core).
Axes of the slice: x: 4 (x_hi: 2, x_lo: 2; x = x_hi * 2 + x_lo), y: 8, z: 8, core: 2. Of those that a mesh axis runs over, the one named last changes fastest.
Arguments:
- seg_queries: bfloat16 [16, 4096, 2048], P('seg', 'tok'), may hold values from -8 to 8
- seg_keys: bfloat16 [16, 4096, 512], P('seg', 'tok'), may hold values from -8 to 8
- seg_values: bfloat16 [16, 4096, 512], P('seg', 'tok'), may hold values from -8 to 8
- grad_out: bfloat16 [16, 4096, 2048], P('seg', 'tok'), may hold values from -6 to 6
- mem_init: float32 [256, 1024], P('tok'), may hold values from -6 to 6
- mem_query: bfloat16 [256, 512], P('tok'), may hold values from -8 to 8
- retention: float32 [16, 1024], P('seg'), may hold values from 0 to 1
- seg_len: int32 [16], replicated, may hold values from 1024 to 4096, as said below
- doc_start: int32 [16], replicated, may hold values from 0 to 1, as said below
Outputs:
- attended: bfloat16 [16, 4096, 2048], P('seg', 'tok')
- memory_in: float32 [16, 256, 1024], P('seg', 'tok')
- memory_grad: float32 [16, 256, 1024], P('seg', 'tok')
The draws below stay inside these ranges and needn't reach their ends.
Inputs may be any that keep to these rules, and one draw needn't show every extreme that they name: `seg_len`: A segment is full unless it is the last one of its document; segment 0 is always full and the last segment is the last one of its document. `doc_start`: segment 0 begins a document and segment 1 never does; any later segment may.
All inputs are finite; a program needn't handle non-finite values.
Results may differ from the reference program's by a relative error of at most 0.009.
Values may be sent and summed in bfloat16 or wider, within the bound.
No kernel may reach another device: no remote copies, remote signals or barrier semaphores. Data moves between devices by JAX's collectives and lax.ppermute only.
A program may use at most 64 MiB of HBM per device.

```python
import math
import jax
import jax.numpy as jnp
from jax import lax

HD = 128
QH = 16
KVH = 4
MEM = 256
GROUP = 4
QW = 2048
KVW = 512
SEGMENT_COUNT = 16
SEG = 4096


def doc_bits(key):
    positions = jnp.arange(SEGMENT_COUNT)
    picks = jax.random.randint(jax.random.fold_in(key, 11), (SEGMENT_COUNT,), 0, SEGMENT_COUNT)
    starts = (positions == 0) | (positions >= 2) & (picks < 2)
    return starts.astype(jnp.int32)


def draw_seg_queries(key, part):
    drawn = jax.random.normal(jax.random.fold_in(key, 1), (SEGMENT_COUNT, SEG, QH, HD), jnp.float32)
    return jnp.clip(drawn, -8.0, 8.0).reshape(SEGMENT_COUNT, SEG, QH * HD).astype(jnp.bfloat16)


def draw_seg_keys(key, part):
    drawn = jax.random.normal(jax.random.fold_in(key, 2), (SEGMENT_COUNT, SEG, KVH, HD), jnp.float32)
    return jnp.clip(drawn, -8.0, 8.0).reshape(SEGMENT_COUNT, SEG, KVH * HD).astype(jnp.bfloat16)


def draw_seg_values(key, part):
    drawn = jax.random.normal(jax.random.fold_in(key, 3), (SEGMENT_COUNT, SEG, KVH * HD), jnp.float32)
    return jnp.clip(drawn, -8.0, 8.0).astype(jnp.bfloat16)


def draw_mem_query(key, part):
    drawn = jax.random.normal(jax.random.fold_in(key, 5), (MEM, KVH, HD), jnp.float32)
    return jnp.clip(drawn, -8.0, 8.0).reshape(MEM, KVH * HD).astype(jnp.bfloat16)


def draw_retention(key, part):
    total_width = 2 * KVH * HD
    slow_share = 0.5
    slow_mask = jax.random.uniform(jax.random.fold_in(key, 20), (1, total_width)) < slow_share
    gradual_decay_rate = jax.random.uniform(jax.random.fold_in(key, 21), (1, total_width), jnp.float32, 0.2, 0.8) / SEGMENT_COUNT
    multiplier = jax.random.uniform(jax.random.fold_in(key, 22), (SEGMENT_COUNT, total_width), jnp.float32, 0.7, 1.4)
    fast_rate = jax.random.uniform(jax.random.fold_in(key, 23), (SEGMENT_COUNT, total_width), jnp.float32, 0.02, 0.3)
    surge_position = jax.random.permutation(jax.random.fold_in(key, 24), SEGMENT_COUNT)[:2]
    surge_row_list = jnp.any(jnp.arange(SEGMENT_COUNT)[:, None] == surge_position[None, :], axis=1)
    surge_retained = jax.random.uniform(jax.random.fold_in(key, 25), (SEGMENT_COUNT, total_width), jnp.float32, 0.65, 0.8)
    retained_entries = jnp.exp(-gradual_decay_rate * multiplier) * jnp.where(surge_row_list[:, None], surge_retained, 1.0)
    return jnp.where(slow_mask, retained_entries, fast_rate)


def draw_doc_start(key, part):
    return doc_bits(key)


def draw_seg_len(key, part):
    positions = jnp.arange(SEGMENT_COUNT)
    starts = doc_bits(key)
    following = jnp.concatenate([starts[1:], jnp.ones((1,), jnp.int32)])
    closing = (following == 1) | (positions == SEGMENT_COUNT - 1)
    ragged = jax.random.randint(jax.random.fold_in(key, 12), (SEGMENT_COUNT,), SEG // 4, SEG + 1)
    return jnp.where(closing, ragged, SEG).astype(jnp.int32)


def steps_of(own_key, dims, pieces, least, high):
    level, own = 1.0, jax.random.fold_in(own_key, 6)
    for position, shards_of in pieces:
        heights = jnp.exp(jax.random.uniform(jax.random.fold_in(own, position), (shards_of,), jnp.float32, least / len(pieces), high / len(pieces)))
        level = level * jnp.repeat(heights, dims[position] // shards_of).reshape([-1 if axis == position else 1 for axis in range(len(dims))])
    return level


def centred(own_key, shape, width, reach, split=(), dtype=jnp.bfloat16):
    values = width * jax.random.normal(own_key, shape, jnp.float32)
    if split:
        values = values * steps_of(own_key, shape, split, -0.22, 0.18)
    return jnp.clip(values, -reach, reach).astype(dtype)


def setup_inputs(seed: int = 0) -> dict:
    keys = jax.random.split(jax.random.key(seed), 10)
    return {
        "seg_queries": draw_seg_queries(jax.random.fold_in(keys[9], 71), 0),
        "seg_keys": draw_seg_keys(jax.random.fold_in(keys[9], 71), 0),
        "seg_values": draw_seg_values(jax.random.fold_in(keys[9], 71), 0),
        "grad_out": centred(keys[3], (SEGMENT_COUNT, SEG, QW), 1.0, 6.0, ((0, 16), (1, 32))),
        "mem_init": centred(keys[4], (MEM, 2 * KVW), 1.0, 6.0, ((0, 32),), jnp.float32),
        "mem_query": draw_mem_query(jax.random.fold_in(keys[9], 71), 0),
        "retention": draw_retention(jax.random.fold_in(keys[9], 71), 0),
        "seg_len": draw_seg_len(jax.random.fold_in(keys[9], 71), 0),
        "doc_start": draw_doc_start(jax.random.fold_in(keys[9], 71), 0),
    }


loss_scale = 16.0
neg_fill = -1e+30
norm_eps = 1e-06

def rounded(values_in):
    narrow = lax.optimization_barrier(values_in.astype(jnp.bfloat16))
    return narrow.astype(jnp.float32)

def slot_norm(raw_rows):
    parts = raw_rows.reshape(raw_rows.shape[0], 2 * KVH, HD)
    multiplier = lax.rsqrt(lax.optimization_barrier(jnp.mean(parts * parts, axis=-1, keepdims=True)) + norm_eps)
    return (parts * multiplier).reshape(raw_rows.shape)

def write_slots(mem_query, key_rows, value_rows, length):
    score_scale = 1.0 / math.sqrt(HD)
    slot_queries = mem_query.astype(jnp.float32).reshape(MEM, KVH, HD)
    key_heads = key_rows.astype(jnp.float32).reshape(SEG, KVH, HD)
    value_heads = value_rows.astype(jnp.float32).reshape(SEG, KVH, HD)
    scores = jnp.einsum('rgd,ugd->gru', slot_queries, key_heads) * score_scale
    live_keys = jnp.arange(SEG) < length
    scores = jnp.where(live_keys, scores, neg_fill)
    row_top = lax.optimization_barrier(jnp.max(scores, axis=-1, keepdims=True))
    weights = jnp.where(live_keys, jnp.exp(scores - row_top), 0.0)
    slot_total = jnp.transpose(lax.optimization_barrier(jnp.sum(weights, axis=-1)))[..., None]
    weights_bf = rounded(weights)
    got_keys = jnp.einsum('gru,ugd->rgd', weights_bf, key_heads) / slot_total
    got_values = jnp.einsum('gru,ugd->rgd', weights_bf, value_heads) / slot_total
    raw_slots = jnp.concatenate([got_keys.reshape(MEM, KVW), got_values.reshape(MEM, KVW)], axis=1)
    return slot_norm(raw_slots)

def segment_pass(query_rows, key_rows, value_rows, grad_rows, memory_now, length):
    score_scale = 1.0 / math.sqrt(HD)
    block_rows = math.gcd(SEG, 512)
    memory_bf = rounded(memory_now)
    mem_keys = memory_bf[:, :KVW].reshape(MEM, KVH, HD)
    mem_vals = memory_bf[:, KVW:].reshape(MEM, KVH, HD)
    grad_keys = jnp.zeros((MEM, KVH, HD), jnp.float32)
    grad_vals = jnp.zeros((MEM, KVH, HD), jnp.float32)
    outputs = []
    for block_index in range(SEG // block_rows):
        first_row = block_index * block_rows
        end_row = first_row + block_rows
        queries = query_rows[first_row:end_row].astype(jnp.float32).reshape(block_rows, KVH, GROUP, HD)
        key_heads = key_rows[:end_row].astype(jnp.float32).reshape(end_row, KVH, HD)
        value_heads = value_rows[:end_row].astype(jnp.float32).reshape(end_row, KVH, HD)
        positions = jnp.arange(first_row, end_row)
        columns = jnp.arange(end_row)
        allowed = (columns[None, :] <= positions[:, None]) & (columns < length)[None, :]
        seg_scores = jnp.einsum('tgjd,ugd->gjtu', queries, key_heads) * score_scale
        seg_scores = jnp.where(allowed, seg_scores, neg_fill)
        mem_scores = jnp.einsum('tgjd,mgd->gjtm', queries, mem_keys) * score_scale
        row_top = jnp.maximum(lax.optimization_barrier(jnp.max(seg_scores, axis=-1)), lax.optimization_barrier(jnp.max(mem_scores, axis=-1)))
        seg_weights = jnp.where(allowed, jnp.exp(seg_scores - row_top[..., None]), 0.0)
        mem_weights = jnp.exp(mem_scores - row_top[..., None])
        row_total = lax.optimization_barrier(jnp.sum(seg_weights, axis=-1)) + lax.optimization_barrier(jnp.sum(mem_weights, axis=-1))
        weighted = jnp.einsum('gjtu,ugd->tgjd', rounded(seg_weights), value_heads)
        weighted = weighted + jnp.einsum('gjtm,mgd->tgjd', rounded(mem_weights), mem_vals)
        att_rows = weighted / jnp.transpose(row_total, (2, 0, 1))[..., None]
        log_total = row_top + jnp.log(row_total)
        outputs.append(att_rows.reshape(block_rows, QW).astype(jnp.bfloat16))
        valid_rows = (positions < length).astype(jnp.float32)[:, None]
        cotangent = (grad_rows[first_row:end_row].astype(jnp.float32) * valid_rows * loss_scale).reshape(block_rows, KVH, GROUP, HD)
        row_delta = jnp.einsum('tgjd,tgjd->gjt', cotangent, att_rows)
        mem_prob = jnp.exp(mem_scores - log_total[..., None])
        grad_prob = jnp.einsum('tgjd,mgd->gjtm', cotangent, mem_vals)
        grad_score = mem_prob * (grad_prob - row_delta[..., None])
        grad_vals = grad_vals + jnp.einsum('gjtm,tgjd->mgd', rounded(mem_prob), cotangent)
        grad_keys = grad_keys + jnp.einsum('gjtm,tgjd->mgd', rounded(grad_score), queries)
    grad_slots = jnp.concatenate([(grad_keys * score_scale).reshape(MEM, KVW), grad_vals.reshape(MEM, KVW)], axis=1)
    return (jnp.concatenate(outputs, axis=0), grad_slots)

def reference(seg_queries, seg_keys, seg_values, grad_out, mem_init, mem_query, retention, seg_len, doc_start):
    written = lax.map(lambda operands: write_slots(mem_query, operands[0], operands[1], operands[2]), (seg_keys, seg_values, seg_len))
    following = jnp.concatenate([doc_start[1:], jnp.zeros((1,), jnp.int32)])
    keep_flag = 1.0 - following.astype(jnp.float32)
    decay_rate = keep_flag[:, None] * retention
    memory_now = mem_init
    states = []
    for segment in range(SEGMENT_COUNT):
        states.append(memory_now)
        carried = keep_flag[segment] * (1.0 - retention[segment]) * written[segment] + (1.0 - keep_flag[segment]) * mem_init
        memory_now = decay_rate[segment] * memory_now + carried
    memory_in = jnp.stack(states)
    attended, local_grad = lax.map(lambda operands: segment_pass(operands[0], operands[1], operands[2], operands[3], operands[4], operands[5]), (seg_queries, seg_keys, seg_values, grad_out, memory_in, seg_len))
    grad_next = jnp.zeros_like(mem_init)
    grads = []
    for segment in range(SEGMENT_COUNT - 1, -1, -1):
        grad_next = local_grad[segment] + decay_rate[segment] * grad_next
        grads.append(grad_next)
    memory_grad = jnp.stack(grads[::-1])
    return (attended, memory_in, memory_grad)
```

```python
import math

import jax
import jax.numpy as jnp
from jax import lax
from jax.sharding import PartitionSpec as P

HD = 128
QH = 16
KVH = 4


loss_scale = 16.0
neg_fill = -1e30
norm_eps = 1e-06


def slot_norm(raw_rows):
    parts = raw_rows.reshape(raw_rows.shape[0], 2 * KVH, HD)
    multiplier = lax.rsqrt(jnp.mean(parts * parts, axis=-1, keepdims=True) + norm_eps)
    return (parts * multiplier).reshape(raw_rows.shape)


def softmax_step(row_top, row_total, scores, allowed):
    scores = jnp.where(allowed, scores, neg_fill)
    new_top = jnp.maximum(row_top, jnp.max(scores, axis=-1))
    weights = jnp.where(allowed, jnp.exp(scores - new_top[..., None]), 0.0)
    multiplier = jnp.exp(row_top - new_top)
    new_total = row_total * multiplier + jnp.sum(weights, axis=-1)
    return (new_top, new_total, weights.astype(jnp.bfloat16), multiplier)


def shards(
    seg_queries, seg_keys, seg_values, grad_out, mem_init, mem_query, retention, seg_len, doc_start
):
    tok_rows = seg_queries.shape[1]
    mem_rows = mem_query.shape[0]
    group_size = QH // KVH
    width_kv = KVH * HD
    seg_count = lax.axis_size("seg")
    seg_index = lax.axis_index("seg")
    tok_index = lax.axis_index("tok")
    length = seg_len[seg_index]
    score_scale = 1.0 / math.sqrt(HD)
    queries = seg_queries[0].reshape(tok_rows, KVH, group_size, HD)
    slot_queries = mem_query.reshape(mem_rows, KVH, HD)
    row_pos = tok_index * tok_rows + jnp.arange(tok_rows)

    kv_piece = lax.all_gather(
        jnp.concatenate([seg_keys[0], seg_values[0]], axis=1), "tok", axis=0, tiled=True
    )
    piece_rows = kv_piece.shape[0]
    key_piece = kv_piece[:, :width_kv].reshape(piece_rows, KVH, HD)
    value_piece = kv_piece[:, width_kv:].reshape(piece_rows, KVH, HD)

    live_keys = jnp.arange(piece_rows) < length
    slot_scores = (
        jnp.einsum("rgd,ugd->gru", slot_queries, key_piece, preferred_element_type=jnp.float32)
        * score_scale
    )
    slot_scores = jnp.where(live_keys, slot_scores, neg_fill)
    slot_top = jnp.max(slot_scores, axis=-1, keepdims=True)
    slot_exp = jnp.where(live_keys, jnp.exp(slot_scores - slot_top), 0.0)
    slot_denom = jnp.transpose(jnp.sum(slot_exp, axis=-1))[..., None]
    slot_weights = slot_exp.astype(jnp.bfloat16)
    slot_keys = jnp.einsum(
        "gru,ugd->rgd", slot_weights, key_piece, preferred_element_type=jnp.float32
    )
    slot_values = jnp.einsum(
        "gru,ugd->rgd", slot_weights, value_piece, preferred_element_type=jnp.float32
    )
    raw_slots = jnp.concatenate(
        [
            (slot_keys / slot_denom).reshape(mem_rows, width_kv),
            (slot_values / slot_denom).reshape(mem_rows, width_kv),
        ],
        axis=1,
    )
    written = slot_norm(raw_slots)
    ret_row = retention[0]
    following = doc_start[jnp.minimum(seg_index + 1, seg_count - 1)].astype(jnp.float32)
    keep_flag = jnp.where(seg_index == seg_count - 1, 1.0, 1.0 - following)
    decay_rate = keep_flag * ret_row
    carried = keep_flag * (1.0 - ret_row) * written + (1.0 - keep_flag) * mem_init

    chain_terms = lax.all_gather(
        jnp.concatenate([carried, decay_rate[None]], axis=0), "seg", axis=0, tiled=False
    )
    all_carried = chain_terms[:, :mem_rows]
    all_decay = chain_terms[:, mem_rows]
    memory_in = mem_init
    for step in range(seg_count - 1):
        following_memory = all_decay[step] * memory_in + all_carried[step]
        memory_in = jnp.where(step < seg_index, following_memory, memory_in)

    block_rows = math.gcd(piece_rows, 512)
    blocks = piece_rows // block_rows
    key_blocks = key_piece.reshape(blocks, block_rows, KVH, HD)
    value_blocks = value_piece.reshape(blocks, block_rows, KVH, HD)
    block_first = block_rows * jnp.arange(blocks)
    starting = (
        jnp.full((KVH, group_size, tok_rows), neg_fill, jnp.float32),
        jnp.zeros((KVH, group_size, tok_rows), jnp.float32),
        jnp.zeros((tok_rows, KVH, group_size, HD), jnp.float32),
    )

    def one_block(inner_state, inputs):
        key_block, value_block, block_start = inputs
        columns = block_start + jnp.arange(block_rows)
        causal = (columns[None, :] <= row_pos[:, None]) & (columns < length)[None, :]
        seg_scores = (
            jnp.einsum("tgjd,ugd->gjtu", queries, key_block, preferred_element_type=jnp.float32)
            * score_scale
        )
        seg_top, seg_total, seg_weights, seg_factor = softmax_step(
            inner_state[0], inner_state[1], seg_scores, causal
        )
        seg_acc = inner_state[2] * jnp.transpose(seg_factor, (2, 0, 1))[..., None] + jnp.einsum(
            "gjtu,ugd->tgjd", seg_weights, value_block, preferred_element_type=jnp.float32
        )
        return ((seg_top, seg_total, seg_acc), None)

    running, _ = lax.scan(one_block, starting, (key_blocks, value_blocks, block_first))

    memory_all = lax.all_gather(memory_in.astype(jnp.bfloat16), "tok", axis=0, tiled=True)
    mem_keys = memory_all[:, :width_kv].reshape(-1, KVH, HD)
    mem_vals = memory_all[:, width_kv:].reshape(-1, KVH, HD)
    mem_scores = (
        jnp.einsum("tgjd,mgd->gjtm", queries, mem_keys, preferred_element_type=jnp.float32)
        * score_scale
    )
    row_top = jnp.maximum(running[0], jnp.max(mem_scores, axis=-1))
    seg_factor = jnp.exp(running[0] - row_top)
    mem_weights = jnp.exp(mem_scores - row_top[..., None])
    row_total = running[1] * seg_factor + jnp.sum(mem_weights, axis=-1)
    weighted = running[2] * jnp.transpose(seg_factor, (2, 0, 1))[..., None] + jnp.einsum(
        "gjtm,mgd->tgjd",
        mem_weights.astype(jnp.bfloat16),
        mem_vals,
        preferred_element_type=jnp.float32,
    )
    att_rows = weighted / jnp.transpose(row_total, (2, 0, 1))[..., None]
    log_total = row_top + jnp.log(row_total)
    attended = att_rows.reshape(1, tok_rows, QH * HD).astype(jnp.bfloat16)
    valid_rows = (row_pos < length).astype(jnp.bfloat16)[:, None]
    cotangent = (grad_out[0] * valid_rows * loss_scale).reshape(tok_rows, KVH, group_size, HD)
    row_delta = jnp.einsum("tgjd,tgjd->gjt", cotangent.astype(jnp.float32), att_rows)
    mem_prob = jnp.exp(mem_scores - log_total[..., None])
    grad_prob = jnp.einsum(
        "tgjd,mgd->gjtm", cotangent, mem_vals, preferred_element_type=jnp.float32
    )
    grad_score = mem_prob * (grad_prob - row_delta[..., None])
    grad_vals = jnp.einsum(
        "gjtm,tgjd->mgd",
        mem_prob.astype(jnp.bfloat16),
        cotangent,
        preferred_element_type=jnp.float32,
    )
    grad_keys = (
        jnp.einsum(
            "gjtm,tgjd->mgd",
            grad_score.astype(jnp.bfloat16),
            queries,
            preferred_element_type=jnp.float32,
        )
        * score_scale
    )
    grad_slots = jnp.concatenate(
        [grad_keys.reshape(-1, width_kv), grad_vals.reshape(-1, width_kv)], axis=1
    )
    local_grad = lax.psum_scatter(grad_slots, "tok", scatter_dimension=0, tiled=True)

    all_local = lax.all_gather(local_grad, "seg", axis=0, tiled=False)
    memory_grad = all_local[seg_count - 1]
    for step in range(seg_count - 2, -1, -1):
        earlier_grad = all_local[step] + all_decay[step] * memory_grad
        memory_grad = jnp.where(step >= seg_index, earlier_grad, memory_grad)
    return (attended, memory_in[None], memory_grad[None])


def solution(mesh):
    placed = (
        P("seg", "tok", None),
        P("seg", "tok", None),
        P("seg", "tok", None),
        P("seg", "tok", None),
        P("tok", None),
        P("tok", None),
        P("seg", None),
        P(),
        P(),
    )
    return jax.shard_map(
        shards,
        mesh=mesh,
        in_specs=placed,
        out_specs=(P("seg", "tok", None), P("seg", "tok", None), P("seg", "tok", None)),
        check_vma=False,
    )
```

```python
import math

import jax
import jax.numpy as jnp
from jax import lax
from jax.sharding import PartitionSpec as P

HD = 128
QH = 16
KVH = 4


loss_scale = 16.0
neg_fill = -1e30
norm_eps = 1e-06


def gathered(block, axis, bits):
    size = lax.axis_size(axis)
    index = lax.axis_index(axis)
    held = block[None]
    for bit in bits:
        partner = [(i, i ^ (1 << bit)) for i in range(size)]
        other = lax.ppermute(held, axis, partner)
        upper = ((index >> bit) & 1) == 1
        held = jnp.stack([jnp.where(upper, other, held), jnp.where(upper, held, other)])
    order = sorted(range(len(bits)), key=lambda k: -bits[k])
    held = jnp.transpose(held, [len(bits) - 1 - k for k in order] + list(range(len(bits), held.ndim)))
    return held.reshape((size,) + block.shape)


def scattered_sum(rows, axis, bits):
    size = lax.axis_size(axis)
    index = lax.axis_index(axis)
    held = rows.reshape((size, rows.shape[0] // size) + rows.shape[1:])
    for bit in bits:
        held = held.reshape((held.shape[0] // 2, 2) + held.shape[1:])
        upper = ((index >> bit) & 1) == 1
        keep = jnp.where(upper, held[:, 1], held[:, 0])
        send = jnp.where(upper, held[:, 0], held[:, 1])
        partner = [(i, i ^ (1 << bit)) for i in range(size)]
        held = keep + lax.ppermute(send, axis, partner)
    return held[0]


def slot_norm(raw_rows):
    parts = raw_rows.reshape(raw_rows.shape[0], 2 * KVH, HD)
    multiplier = lax.rsqrt(jnp.mean(parts * parts, axis=-1, keepdims=True) + norm_eps)
    return (parts * multiplier).reshape(raw_rows.shape)


def softmax_step(row_top, row_total, scores, allowed):
    scores = jnp.where(allowed, scores, neg_fill)
    new_top = jnp.maximum(row_top, jnp.max(scores, axis=-1))
    weights = jnp.where(allowed, jnp.exp(scores - new_top[..., None]), 0.0)
    multiplier = jnp.exp(row_top - new_top)
    new_total = row_total * multiplier + jnp.sum(weights, axis=-1)
    return (new_top, new_total, weights.astype(jnp.bfloat16), multiplier)


def shards(
    seg_queries, seg_keys, seg_values, grad_out, mem_init, mem_query, retention, seg_len, doc_start
):
    tok_rows = seg_queries.shape[1]
    mem_rows = mem_query.shape[0]
    group_size = QH // KVH
    width_kv = KVH * HD
    seg_count = lax.axis_size("seg")
    seg_index = lax.axis_index("seg")
    tok_index = lax.axis_index("tok")
    length = seg_len[seg_index]
    score_scale = 1.0 / math.sqrt(HD)
    queries = seg_queries[0].reshape(tok_rows, KVH, group_size, HD)
    slot_queries = mem_query.reshape(mem_rows, KVH, HD)
    row_pos = tok_index * tok_rows + jnp.arange(tok_rows)

    kv_piece = lax.all_gather(
        jnp.concatenate([seg_keys[0], seg_values[0]], axis=1), "tok", axis=0, tiled=True
    )
    piece_rows = kv_piece.shape[0]
    key_piece = kv_piece[:, :width_kv].reshape(piece_rows, KVH, HD)
    value_piece = kv_piece[:, width_kv:].reshape(piece_rows, KVH, HD)

    live_keys = jnp.arange(piece_rows) < length
    slot_scores = (
        jnp.einsum("rgd,ugd->gru", slot_queries, key_piece, preferred_element_type=jnp.float32)
        * score_scale
    )
    slot_scores = jnp.where(live_keys, slot_scores, neg_fill)
    slot_top = jnp.max(slot_scores, axis=-1, keepdims=True)
    slot_exp = jnp.where(live_keys, jnp.exp(slot_scores - slot_top), 0.0)
    slot_denom = jnp.transpose(jnp.sum(slot_exp, axis=-1))[..., None]
    slot_weights = slot_exp.astype(jnp.bfloat16)
    slot_keys = jnp.einsum(
        "gru,ugd->rgd", slot_weights, key_piece, preferred_element_type=jnp.float32
    )
    slot_values = jnp.einsum(
        "gru,ugd->rgd", slot_weights, value_piece, preferred_element_type=jnp.float32
    )
    raw_slots = jnp.concatenate(
        [
            (slot_keys / slot_denom).reshape(mem_rows, width_kv),
            (slot_values / slot_denom).reshape(mem_rows, width_kv),
        ],
        axis=1,
    )
    written = slot_norm(raw_slots)
    ret_row = retention[0]
    following = doc_start[jnp.minimum(seg_index + 1, seg_count - 1)].astype(jnp.float32)
    keep_flag = jnp.where(seg_index == seg_count - 1, 1.0, 1.0 - following)
    decay_rate = keep_flag * ret_row
    carried = keep_flag * (1.0 - ret_row) * written + (1.0 - keep_flag) * mem_init

    chain_terms = gathered(
        jnp.concatenate([carried, decay_rate[None]], axis=0), "seg", (3, 2, 1, 0)
    )
    all_carried = chain_terms[:, :mem_rows]
    all_decay = chain_terms[:, mem_rows]
    memory_in = mem_init
    for step in range(seg_count - 1):
        following_memory = all_decay[step] * memory_in + all_carried[step]
        memory_in = jnp.where(step < seg_index, following_memory, memory_in)

    block_rows = math.gcd(piece_rows, 512)
    blocks = piece_rows // block_rows
    key_blocks = key_piece.reshape(blocks, block_rows, KVH, HD)
    value_blocks = value_piece.reshape(blocks, block_rows, KVH, HD)
    block_first = block_rows * jnp.arange(blocks)
    starting = (
        jnp.full((KVH, group_size, tok_rows), neg_fill, jnp.float32),
        jnp.zeros((KVH, group_size, tok_rows), jnp.float32),
        jnp.zeros((tok_rows, KVH, group_size, HD), jnp.float32),
    )

    def one_block(inner_state, inputs):
        key_block, value_block, block_start = inputs
        columns = block_start + jnp.arange(block_rows)
        causal = (columns[None, :] <= row_pos[:, None]) & (columns < length)[None, :]
        seg_scores = (
            jnp.einsum("tgjd,ugd->gjtu", queries, key_block, preferred_element_type=jnp.float32)
            * score_scale
        )
        seg_top, seg_total, seg_weights, seg_factor = softmax_step(
            inner_state[0], inner_state[1], seg_scores, causal
        )
        seg_acc = inner_state[2] * jnp.transpose(seg_factor, (2, 0, 1))[..., None] + jnp.einsum(
            "gjtu,ugd->tgjd", seg_weights, value_block, preferred_element_type=jnp.float32
        )
        return ((seg_top, seg_total, seg_acc), None)

    running, _ = lax.scan(one_block, starting, (key_blocks, value_blocks, block_first))

    memory_all = gathered(memory_in.astype(jnp.bfloat16), "tok", (4, 3, 2, 1, 0)).reshape(
        -1, 2 * width_kv
    )
    mem_keys = memory_all[:, :width_kv].reshape(-1, KVH, HD)
    mem_vals = memory_all[:, width_kv:].reshape(-1, KVH, HD)
    mem_scores = (
        jnp.einsum("tgjd,mgd->gjtm", queries, mem_keys, preferred_element_type=jnp.float32)
        * score_scale
    )
    row_top = jnp.maximum(running[0], jnp.max(mem_scores, axis=-1))
    seg_factor = jnp.exp(running[0] - row_top)
    mem_weights = jnp.exp(mem_scores - row_top[..., None])
    row_total = running[1] * seg_factor + jnp.sum(mem_weights, axis=-1)
    weighted = running[2] * jnp.transpose(seg_factor, (2, 0, 1))[..., None] + jnp.einsum(
        "gjtm,mgd->tgjd",
        mem_weights.astype(jnp.bfloat16),
        mem_vals,
        preferred_element_type=jnp.float32,
    )
    att_rows = weighted / jnp.transpose(row_total, (2, 0, 1))[..., None]
    log_total = row_top + jnp.log(row_total)
    attended = att_rows.reshape(1, tok_rows, QH * HD).astype(jnp.bfloat16)
    valid_rows = (row_pos < length).astype(jnp.bfloat16)[:, None]
    cotangent = (grad_out[0] * valid_rows * loss_scale).reshape(tok_rows, KVH, group_size, HD)
    row_delta = jnp.einsum("tgjd,tgjd->gjt", cotangent.astype(jnp.float32), att_rows)
    mem_prob = jnp.exp(mem_scores - log_total[..., None])
    grad_prob = jnp.einsum(
        "tgjd,mgd->gjtm", cotangent, mem_vals, preferred_element_type=jnp.float32
    )
    grad_score = mem_prob * (grad_prob - row_delta[..., None])
    grad_vals = jnp.einsum(
        "gjtm,tgjd->mgd",
        mem_prob.astype(jnp.bfloat16),
        cotangent,
        preferred_element_type=jnp.float32,
    )
    grad_keys = (
        jnp.einsum(
            "gjtm,tgjd->mgd",
            grad_score.astype(jnp.bfloat16),
            queries,
            preferred_element_type=jnp.float32,
        )
        * score_scale
    )
    grad_slots = jnp.concatenate(
        [grad_keys.reshape(-1, width_kv), grad_vals.reshape(-1, width_kv)], axis=1
    )
    local_grad = scattered_sum(grad_slots, "tok", (0, 1, 2, 3, 4))

    all_local = gathered(local_grad, "seg", (3, 2, 1, 0))
    memory_grad = all_local[seg_count - 1]
    for step in range(seg_count - 2, -1, -1):
        earlier_grad = all_local[step] + all_decay[step] * memory_grad
        memory_grad = jnp.where(step >= seg_index, earlier_grad, memory_grad)
    return (attended, memory_in[None], memory_grad[None])


def solution(mesh):
    placed = (
        P("seg", "tok", None),
        P("seg", "tok", None),
        P("seg", "tok", None),
        P("seg", "tok", None),
        P("tok", None),
        P("tok", None),
        P("seg", None),
        P(),
        P(),
    )
    return jax.shard_map(
        shards,
        mesh=mesh,
        in_specs=placed,
        out_specs=(P("seg", "tok", None), P("seg", "tok", None), P("seg", "tok", None)),
        check_vma=False,
    )
```

```python
import math

import jax
import jax.numpy as jnp
from jax import lax
from jax.sharding import PartitionSpec as P

HD = 128
QH = 16
KVH = 4


loss_scale = 16.0
neg_fill = -1e30
norm_eps = 1e-06


def gathered(block, axis, bits):
    size = lax.axis_size(axis)
    index = lax.axis_index(axis)
    held = block[None]
    for bit in bits:
        partner = [(i, i ^ (1 << bit)) for i in range(size)]
        other = lax.ppermute(held, axis, partner)
        upper = ((index >> bit) & 1) == 1
        held = jnp.stack([jnp.where(upper, other, held), jnp.where(upper, held, other)])
    order = sorted(range(len(bits)), key=lambda k: -bits[k])
    held = jnp.transpose(held, [len(bits) - 1 - k for k in order] + list(range(len(bits), held.ndim)))
    return held.reshape((size,) + block.shape)


def scattered_sum(rows, axis, bits):
    size = lax.axis_size(axis)
    index = lax.axis_index(axis)
    held = rows.reshape((size, rows.shape[0] // size) + rows.shape[1:])
    for bit in bits:
        held = held.reshape((held.shape[0] // 2, 2) + held.shape[1:])
        upper = ((index >> bit) & 1) == 1
        keep = jnp.where(upper, held[:, 1], held[:, 0])
        send = jnp.where(upper, held[:, 0], held[:, 1])
        partner = [(i, i ^ (1 << bit)) for i in range(size)]
        held = keep + lax.ppermute(send, axis, partner)
    return held[0]


def slot_norm(raw_rows):
    parts = raw_rows.reshape(raw_rows.shape[0], 2 * KVH, HD)
    multiplier = lax.rsqrt(jnp.mean(parts * parts, axis=-1, keepdims=True) + norm_eps)
    return (parts * multiplier).reshape(raw_rows.shape)


def softmax_step(row_top, row_total, scores, allowed):
    scores = jnp.where(allowed, scores, neg_fill)
    new_top = jnp.maximum(row_top, jnp.max(scores, axis=-1))
    weights = jnp.where(allowed, jnp.exp(scores - new_top[..., None]), 0.0)
    multiplier = jnp.exp(row_top - new_top)
    new_total = row_total * multiplier + jnp.sum(weights, axis=-1)
    return (new_top, new_total, weights.astype(jnp.bfloat16), multiplier)


def shards(
    seg_queries, seg_keys, seg_values, grad_out, mem_init, mem_query, retention, seg_len, doc_start
):
    tok_rows = seg_queries.shape[1]
    mem_rows = mem_query.shape[0]
    group_size = QH // KVH
    width_kv = KVH * HD
    seg_count = lax.axis_size("seg")
    seg_index = lax.axis_index("seg")
    tok_index = lax.axis_index("tok")
    length = seg_len[seg_index]
    score_scale = 1.0 / math.sqrt(HD)
    queries = seg_queries[0].reshape(tok_rows, KVH, group_size, HD)
    slot_queries = mem_query.reshape(mem_rows, KVH, HD)
    row_pos = tok_index * tok_rows + jnp.arange(tok_rows)

    kv_piece = lax.all_gather(
        jnp.concatenate([seg_keys[0], seg_values[0]], axis=1), "tok", axis=0, tiled=True
    )
    piece_rows = kv_piece.shape[0]
    key_piece = kv_piece[:, :width_kv].reshape(piece_rows, KVH, HD)
    value_piece = kv_piece[:, width_kv:].reshape(piece_rows, KVH, HD)

    live_keys = jnp.arange(piece_rows) < length
    slot_scores = (
        jnp.einsum("rgd,ugd->gru", slot_queries, key_piece, preferred_element_type=jnp.float32)
        * score_scale
    )
    slot_scores = jnp.where(live_keys, slot_scores, neg_fill)
    slot_top = jnp.max(slot_scores, axis=-1, keepdims=True)
    slot_exp = jnp.where(live_keys, jnp.exp(slot_scores - slot_top), 0.0)
    slot_denom = jnp.transpose(jnp.sum(slot_exp, axis=-1))[..., None]
    slot_weights = slot_exp.astype(jnp.bfloat16)
    slot_keys = jnp.einsum(
        "gru,ugd->rgd", slot_weights, key_piece, preferred_element_type=jnp.float32
    )
    slot_values = jnp.einsum(
        "gru,ugd->rgd", slot_weights, value_piece, preferred_element_type=jnp.float32
    )
    raw_slots = jnp.concatenate(
        [
            (slot_keys / slot_denom).reshape(mem_rows, width_kv),
            (slot_values / slot_denom).reshape(mem_rows, width_kv),
        ],
        axis=1,
    )
    written = slot_norm(raw_slots)
    ret_row = retention[0]
    following = doc_start[jnp.minimum(seg_index + 1, seg_count - 1)].astype(jnp.float32)
    keep_flag = jnp.where(seg_index == seg_count - 1, 1.0, 1.0 - following)
    decay_rate = keep_flag * ret_row
    carried = keep_flag * (1.0 - ret_row) * written + (1.0 - keep_flag) * mem_init

    chain_terms = gathered(
        jnp.concatenate([carried, decay_rate[None]], axis=0), "seg", (3, 2, 1, 0)
    )
    all_carried = chain_terms[:, :mem_rows]
    all_decay = chain_terms[:, mem_rows]
    memory_in = mem_init
    for step in range(seg_count - 1):
        following_memory = all_decay[step] * memory_in + all_carried[step]
        memory_in = jnp.where(step < seg_index, following_memory, memory_in)

    block_rows = math.gcd(piece_rows, 512)
    blocks = piece_rows // block_rows
    running = (
        jnp.full((KVH, group_size, tok_rows), neg_fill, jnp.float32),
        jnp.zeros((KVH, group_size, tok_rows), jnp.float32),
        jnp.zeros((tok_rows, KVH, group_size, HD), jnp.float32),
    )
    for block in range(blocks):
        block_start = block * block_rows
        key_block = key_piece[block_start : block_start + block_rows]
        value_block = value_piece[block_start : block_start + block_rows]
        columns = block_start + jnp.arange(block_rows)
        causal = (columns[None, :] <= row_pos[:, None]) & (columns < length)[None, :]
        seg_scores = (
            jnp.einsum("tgjd,ugd->gjtu", queries, key_block, preferred_element_type=jnp.float32)
            * score_scale
        )
        seg_top, seg_total, seg_weights, seg_factor = softmax_step(
            running[0], running[1], seg_scores, causal
        )
        seg_acc = running[2] * jnp.transpose(seg_factor, (2, 0, 1))[..., None] + jnp.einsum(
            "gjtu,ugd->tgjd", seg_weights, value_block, preferred_element_type=jnp.float32
        )
        running = (seg_top, seg_total, seg_acc)

    memory_all = gathered(memory_in.astype(jnp.bfloat16), "tok", (4, 3, 2, 1, 0)).reshape(
        -1, 2 * width_kv
    )
    mem_keys = memory_all[:, :width_kv].reshape(-1, KVH, HD)
    mem_vals = memory_all[:, width_kv:].reshape(-1, KVH, HD)
    mem_scores = (
        jnp.einsum("tgjd,mgd->gjtm", queries, mem_keys, preferred_element_type=jnp.float32)
        * score_scale
    )
    row_top = jnp.maximum(running[0], jnp.max(mem_scores, axis=-1))
    seg_factor = jnp.exp(running[0] - row_top)
    mem_weights = jnp.exp(mem_scores - row_top[..., None])
    row_total = running[1] * seg_factor + jnp.sum(mem_weights, axis=-1)
    weighted = running[2] * jnp.transpose(seg_factor, (2, 0, 1))[..., None] + jnp.einsum(
        "gjtm,mgd->tgjd",
        mem_weights.astype(jnp.bfloat16),
        mem_vals,
        preferred_element_type=jnp.float32,
    )
    att_rows = weighted / jnp.transpose(row_total, (2, 0, 1))[..., None]
    log_total = row_top + jnp.log(row_total)
    attended = att_rows.reshape(1, tok_rows, QH * HD).astype(jnp.bfloat16)
    valid_rows = (row_pos < length).astype(jnp.bfloat16)[:, None]
    cotangent = (grad_out[0] * valid_rows * loss_scale).reshape(tok_rows, KVH, group_size, HD)
    row_delta = jnp.einsum("tgjd,tgjd->gjt", cotangent.astype(jnp.float32), att_rows)
    mem_prob = jnp.exp(mem_scores - log_total[..., None])
    grad_prob = jnp.einsum(
        "tgjd,mgd->gjtm", cotangent, mem_vals, preferred_element_type=jnp.float32
    )
    grad_score = mem_prob * (grad_prob - row_delta[..., None])
    grad_vals = jnp.einsum(
        "gjtm,tgjd->mgd",
        mem_prob.astype(jnp.bfloat16),
        cotangent,
        preferred_element_type=jnp.float32,
    )
    grad_keys = (
        jnp.einsum(
            "gjtm,tgjd->mgd",
            grad_score.astype(jnp.bfloat16),
            queries,
            preferred_element_type=jnp.float32,
        )
        * score_scale
    )
    grad_slots = jnp.concatenate(
        [grad_keys.reshape(-1, width_kv), grad_vals.reshape(-1, width_kv)], axis=1
    )
    local_grad = scattered_sum(grad_slots, "tok", (0, 1, 2, 3, 4))

    all_local = gathered(local_grad, "seg", (3, 2, 1, 0))
    memory_grad = all_local[seg_count - 1]
    for step in range(seg_count - 2, -1, -1):
        earlier_grad = all_local[step] + all_decay[step] * memory_grad
        memory_grad = jnp.where(step >= seg_index, earlier_grad, memory_grad)
    return (attended, memory_in[None], memory_grad[None])


def solution(mesh):
    placed = (
        P("seg", "tok", None),
        P("seg", "tok", None),
        P("seg", "tok", None),
        P("seg", "tok", None),
        P("tok", None),
        P("tok", None),
        P("seg", None),
        P(),
        P(),
    )
    return jax.shard_map(
        shards,
        mesh=mesh,
        in_specs=placed,
        out_specs=(P("seg", "tok", None), P("seg", "tok", None), P("seg", "tok", None)),
        check_vma=False,
    )
```

```python
import math

import jax
import jax.numpy as jnp
from jax import lax
from jax.sharding import PartitionSpec as P

HD = 128
QH = 16
KVH = 4


loss_scale = 16.0
neg_fill = -1e30
norm_eps = 1e-06


def gathered(block, axis, groups):
    size = lax.axis_size(axis)
    index = lax.axis_index(axis)
    held = block[None]
    axis_bits = []
    for group in groups:
        group = sorted(group)
        mine = sum(((index >> bit) & 1) << k for k, bit in enumerate(group))
        arrived = [held]
        for mask in range(1, 1 << len(group)):
            flip = sum(((mask >> k) & 1) << bit for k, bit in enumerate(group))
            arrived.append(lax.ppermute(held, axis, [(i, i ^ flip) for i in range(size)]))
        placed = []
        for place in range(1 << len(group)):
            value = arrived[0]
            for mask in range(1, 1 << len(group)):
                value = jnp.where((mine ^ mask) == place, arrived[mask], value)
            placed.append(value)
        held = jnp.stack(placed).reshape((2,) * len(group) + held.shape)
        axis_bits = group[::-1] + axis_bits
    order = sorted(range(len(axis_bits)), key=lambda k: -axis_bits[k])
    held = jnp.transpose(held, order + list(range(len(axis_bits), held.ndim)))
    return held.reshape((size,) + block.shape)


def scattered_sum(rows, axis, groups):
    size = lax.axis_size(axis)
    index = lax.axis_index(axis)
    held = rows.reshape((size, rows.shape[0] // size) + rows.shape[1:])
    low = 0
    for width in groups:
        ways = 1 << width
        held = held.reshape((held.shape[0] // ways, ways) + held.shape[1:])
        mine = (index >> low) & (ways - 1)
        total = lax.dynamic_index_in_dim(held, mine, axis=1, keepdims=False)
        for mask in range(1, ways):
            send = lax.dynamic_index_in_dim(held, mine ^ mask, axis=1, keepdims=False)
            flip = mask << low
            total = total + lax.ppermute(send, axis, [(i, i ^ flip) for i in range(size)])
        held = total
        low += width
    return held[0]


def slot_norm(raw_rows):
    parts = raw_rows.reshape(raw_rows.shape[0], 2 * KVH, HD)
    multiplier = lax.rsqrt(jnp.mean(parts * parts, axis=-1, keepdims=True) + norm_eps)
    return (parts * multiplier).reshape(raw_rows.shape)


def softmax_step(row_top, row_total, scores, allowed):
    scores = jnp.where(allowed, scores, neg_fill)
    new_top = jnp.maximum(row_top, jnp.max(scores, axis=-1))
    weights = jnp.where(allowed, jnp.exp(scores - new_top[..., None]), 0.0)
    multiplier = jnp.exp(row_top - new_top)
    new_total = row_total * multiplier + jnp.sum(weights, axis=-1)
    return (new_top, new_total, weights.astype(jnp.bfloat16), multiplier)


def shards(
    seg_queries, seg_keys, seg_values, grad_out, mem_init, mem_query, retention, seg_len, doc_start
):
    tok_rows = seg_queries.shape[1]
    mem_rows = mem_query.shape[0]
    group_size = QH // KVH
    width_kv = KVH * HD
    seg_count = lax.axis_size("seg")
    seg_index = lax.axis_index("seg")
    tok_index = lax.axis_index("tok")
    length = seg_len[seg_index]
    score_scale = 1.0 / math.sqrt(HD)
    queries = seg_queries[0].reshape(tok_rows, KVH, group_size, HD)
    slot_queries = mem_query.reshape(mem_rows, KVH, HD)
    row_pos = tok_index * tok_rows + jnp.arange(tok_rows)

    kv_piece = lax.all_gather(
        jnp.concatenate([seg_keys[0], seg_values[0]], axis=1), "tok", axis=0, tiled=True
    )
    piece_rows = kv_piece.shape[0]
    key_piece = kv_piece[:, :width_kv].reshape(piece_rows, KVH, HD)
    value_piece = kv_piece[:, width_kv:].reshape(piece_rows, KVH, HD)

    live_keys = jnp.arange(piece_rows) < length
    slot_scores = (
        jnp.einsum("rgd,ugd->gru", slot_queries, key_piece, preferred_element_type=jnp.float32)
        * score_scale
    )
    slot_scores = jnp.where(live_keys, slot_scores, neg_fill)
    slot_top = jnp.max(slot_scores, axis=-1, keepdims=True)
    slot_exp = jnp.where(live_keys, jnp.exp(slot_scores - slot_top), 0.0)
    slot_denom = jnp.transpose(jnp.sum(slot_exp, axis=-1))[..., None]
    slot_weights = slot_exp.astype(jnp.bfloat16)
    slot_keys = jnp.einsum(
        "gru,ugd->rgd", slot_weights, key_piece, preferred_element_type=jnp.float32
    )
    slot_values = jnp.einsum(
        "gru,ugd->rgd", slot_weights, value_piece, preferred_element_type=jnp.float32
    )
    raw_slots = jnp.concatenate(
        [
            (slot_keys / slot_denom).reshape(mem_rows, width_kv),
            (slot_values / slot_denom).reshape(mem_rows, width_kv),
        ],
        axis=1,
    )
    written = slot_norm(raw_slots)
    ret_row = retention[0]
    following = doc_start[jnp.minimum(seg_index + 1, seg_count - 1)].astype(jnp.float32)
    keep_flag = jnp.where(seg_index == seg_count - 1, 1.0, 1.0 - following)
    decay_rate = keep_flag * ret_row
    carried = keep_flag * (1.0 - ret_row) * written + (1.0 - keep_flag) * mem_init

    chain_terms = gathered(
        jnp.concatenate([carried, decay_rate[None]], axis=0), "seg", ((2, 3), (0, 1))
    )
    all_carried = chain_terms[:, :mem_rows]
    all_decay = chain_terms[:, mem_rows]
    memory_in = mem_init
    for step in range(seg_count - 1):
        following_memory = all_decay[step] * memory_in + all_carried[step]
        memory_in = jnp.where(step < seg_index, following_memory, memory_in)

    block_rows = math.gcd(piece_rows, 512)
    blocks = piece_rows // block_rows
    running = (
        jnp.full((KVH, group_size, tok_rows), neg_fill, jnp.float32),
        jnp.zeros((KVH, group_size, tok_rows), jnp.float32),
        jnp.zeros((tok_rows, KVH, group_size, HD), jnp.float32),
    )
    for block in range(blocks):
        block_start = block * block_rows
        key_block = key_piece[block_start : block_start + block_rows]
        value_block = value_piece[block_start : block_start + block_rows]
        columns = block_start + jnp.arange(block_rows)
        causal = (columns[None, :] <= row_pos[:, None]) & (columns < length)[None, :]
        seg_scores = (
            jnp.einsum("tgjd,ugd->gjtu", queries, key_block, preferred_element_type=jnp.float32)
            * score_scale
        )
        seg_top, seg_total, seg_weights, seg_factor = softmax_step(
            running[0], running[1], seg_scores, causal
        )
        seg_acc = running[2] * jnp.transpose(seg_factor, (2, 0, 1))[..., None] + jnp.einsum(
            "gjtu,ugd->tgjd", seg_weights, value_block, preferred_element_type=jnp.float32
        )
        running = (seg_top, seg_total, seg_acc)

    memory_all = gathered(memory_in.astype(jnp.bfloat16), "tok", ((3, 4), (1, 2), (0,))).reshape(
        -1, 2 * width_kv
    )
    mem_keys = memory_all[:, :width_kv].reshape(-1, KVH, HD)
    mem_vals = memory_all[:, width_kv:].reshape(-1, KVH, HD)
    mem_scores = (
        jnp.einsum("tgjd,mgd->gjtm", queries, mem_keys, preferred_element_type=jnp.float32)
        * score_scale
    )
    row_top = jnp.maximum(running[0], jnp.max(mem_scores, axis=-1))
    seg_factor = jnp.exp(running[0] - row_top)
    mem_weights = jnp.exp(mem_scores - row_top[..., None])
    row_total = running[1] * seg_factor + jnp.sum(mem_weights, axis=-1)
    weighted = running[2] * jnp.transpose(seg_factor, (2, 0, 1))[..., None] + jnp.einsum(
        "gjtm,mgd->tgjd",
        mem_weights.astype(jnp.bfloat16),
        mem_vals,
        preferred_element_type=jnp.float32,
    )
    att_rows = weighted / jnp.transpose(row_total, (2, 0, 1))[..., None]
    log_total = row_top + jnp.log(row_total)
    attended = att_rows.reshape(1, tok_rows, QH * HD).astype(jnp.bfloat16)
    valid_rows = (row_pos < length).astype(jnp.bfloat16)[:, None]
    cotangent = (grad_out[0] * valid_rows * loss_scale).reshape(tok_rows, KVH, group_size, HD)
    row_delta = jnp.einsum("tgjd,tgjd->gjt", cotangent.astype(jnp.float32), att_rows)
    mem_prob = jnp.exp(mem_scores - log_total[..., None])
    grad_prob = jnp.einsum(
        "tgjd,mgd->gjtm", cotangent, mem_vals, preferred_element_type=jnp.float32
    )
    grad_score = mem_prob * (grad_prob - row_delta[..., None])
    grad_vals = jnp.einsum(
        "gjtm,tgjd->mgd",
        mem_prob.astype(jnp.bfloat16),
        cotangent,
        preferred_element_type=jnp.float32,
    )
    grad_keys = (
        jnp.einsum(
            "gjtm,tgjd->mgd",
            grad_score.astype(jnp.bfloat16),
            queries,
            preferred_element_type=jnp.float32,
        )
        * score_scale
    )
    grad_slots = jnp.concatenate(
        [grad_keys.reshape(-1, width_kv), grad_vals.reshape(-1, width_kv)], axis=1
    )
    local_grad = scattered_sum(grad_slots, "tok", (1, 2, 2))

    all_local = gathered(local_grad, "seg", ((2, 3), (0, 1)))
    memory_grad = all_local[seg_count - 1]
    for step in range(seg_count - 2, -1, -1):
        earlier_grad = all_local[step] + all_decay[step] * memory_grad
        memory_grad = jnp.where(step >= seg_index, earlier_grad, memory_grad)
    return (attended, memory_in[None], memory_grad[None])


def solution(mesh):
    placed = (
        P("seg", "tok", None),
        P("seg", "tok", None),
        P("seg", "tok", None),
        P("seg", "tok", None),
        P("tok", None),
        P("tok", None),
        P("seg", None),
        P(),
        P(),
    )
    return jax.shard_map(
        shards,
        mesh=mesh,
        in_specs=placed,
        out_specs=(P("seg", "tok", None), P("seg", "tok", None), P("seg", "tok", None)),
        check_vma=False,
    )
```

```python
import math

import jax
import jax.numpy as jnp
from jax import lax
from jax.sharding import PartitionSpec as P

HD = 128
QH = 16
KVH = 4


loss_scale = 16.0
neg_fill = -1e30
norm_eps = 1e-06


def gathered(block, axis, groups):
    size = lax.axis_size(axis)
    index = lax.axis_index(axis)
    held = block[None]
    axis_bits = []
    for group in groups:
        group = sorted(group)
        mine = sum(((index >> bit) & 1) << k for k, bit in enumerate(group))
        arrived = [held]
        for mask in range(1, 1 << len(group)):
            flip = sum(((mask >> k) & 1) << bit for k, bit in enumerate(group))
            arrived.append(lax.ppermute(held, axis, [(i, i ^ flip) for i in range(size)]))
        placed = []
        for place in range(1 << len(group)):
            value = arrived[0]
            for mask in range(1, 1 << len(group)):
                value = jnp.where((mine ^ mask) == place, arrived[mask], value)
            placed.append(value)
        held = jnp.stack(placed).reshape((2,) * len(group) + held.shape)
        axis_bits = group[::-1] + axis_bits
    order = sorted(range(len(axis_bits)), key=lambda k: -axis_bits[k])
    held = jnp.transpose(held, order + list(range(len(axis_bits), held.ndim)))
    return held.reshape((size,) + block.shape)


def scattered_sum(rows, axis, groups):
    size = lax.axis_size(axis)
    index = lax.axis_index(axis)
    held = rows.reshape((size, rows.shape[0] // size) + rows.shape[1:])
    low = 0
    for width in groups:
        ways = 1 << width
        held = held.reshape((held.shape[0] // ways, ways) + held.shape[1:])
        mine = (index >> low) & (ways - 1)
        total = lax.dynamic_index_in_dim(held, mine, axis=1, keepdims=False)
        for mask in range(1, ways):
            send = lax.dynamic_index_in_dim(held, mine ^ mask, axis=1, keepdims=False)
            flip = mask << low
            total = total + lax.ppermute(send, axis, [(i, i ^ flip) for i in range(size)])
        held = total
        low += width
    return held[0]


def slot_norm(raw_rows):
    parts = raw_rows.reshape(raw_rows.shape[0], 2 * KVH, HD)
    multiplier = lax.rsqrt(jnp.mean(parts * parts, axis=-1, keepdims=True) + norm_eps)
    return (parts * multiplier).reshape(raw_rows.shape)


def softmax_step(row_top, row_total, scores, allowed):
    scores = jnp.where(allowed, scores, neg_fill)
    new_top = jnp.maximum(row_top, jnp.max(scores, axis=-1))
    weights = jnp.where(allowed, jnp.exp(scores - new_top[..., None]), 0.0)
    multiplier = jnp.exp(row_top - new_top)
    new_total = row_total * multiplier + jnp.sum(weights, axis=-1)
    return (new_top, new_total, weights.astype(jnp.bfloat16), multiplier)


def shards(
    seg_queries, seg_keys, seg_values, grad_out, mem_init, mem_query, retention, seg_len, doc_start
):
    tok_rows = seg_queries.shape[1]
    mem_rows = mem_query.shape[0]
    group_size = QH // KVH
    width_kv = KVH * HD
    seg_count = lax.axis_size("seg")
    seg_index = lax.axis_index("seg")
    tok_index = lax.axis_index("tok")
    length = seg_len[seg_index]
    score_scale = 1.0 / math.sqrt(HD)
    queries = seg_queries[0].reshape(tok_rows, KVH, group_size, HD)
    slot_queries = mem_query.reshape(mem_rows, KVH, HD)
    row_pos = tok_index * tok_rows + jnp.arange(tok_rows)

    kv_piece = lax.all_gather(
        jnp.concatenate([seg_keys[0], seg_values[0]], axis=1), "tok", axis=0, tiled=True
    )
    piece_rows = kv_piece.shape[0]
    key_piece = kv_piece[:, :width_kv].reshape(piece_rows, KVH, HD)
    value_piece = kv_piece[:, width_kv:].reshape(piece_rows, KVH, HD)

    live_keys = jnp.arange(piece_rows) < length
    slot_scores = (
        jnp.einsum("rgd,ugd->gru", slot_queries, key_piece, preferred_element_type=jnp.float32)
        * score_scale
    )
    slot_scores = jnp.where(live_keys, slot_scores, neg_fill)
    slot_top = jnp.max(slot_scores, axis=-1, keepdims=True)
    slot_exp = jnp.where(live_keys, jnp.exp(slot_scores - slot_top), 0.0)
    slot_denom = jnp.transpose(jnp.sum(slot_exp, axis=-1))[..., None]
    slot_weights = slot_exp.astype(jnp.bfloat16)
    slot_keys = jnp.einsum(
        "gru,ugd->rgd", slot_weights, key_piece, preferred_element_type=jnp.float32
    )
    slot_values = jnp.einsum(
        "gru,ugd->rgd", slot_weights, value_piece, preferred_element_type=jnp.float32
    )
    raw_slots = jnp.concatenate(
        [
            (slot_keys / slot_denom).reshape(mem_rows, width_kv),
            (slot_values / slot_denom).reshape(mem_rows, width_kv),
        ],
        axis=1,
    )
    written = slot_norm(raw_slots)
    ret_row = retention[0]
    following = doc_start[jnp.minimum(seg_index + 1, seg_count - 1)].astype(jnp.float32)
    keep_flag = jnp.where(seg_index == seg_count - 1, 1.0, 1.0 - following)
    decay_rate = keep_flag * ret_row
    carried = keep_flag * (1.0 - ret_row) * written + (1.0 - keep_flag) * mem_init

    chain_terms = gathered(
        jnp.concatenate([carried, decay_rate[None]], axis=0), "seg", ((2, 3), (0, 1))
    )
    all_carried = chain_terms[:, :mem_rows]
    all_decay = chain_terms[:, mem_rows]
    memory_in = mem_init
    for step in range(seg_count - 1):
        following_memory = all_decay[step] * memory_in + all_carried[step]
        memory_in = jnp.where(step < seg_index, following_memory, memory_in)

    block_rows = math.gcd(piece_rows, 512)
    blocks = piece_rows // block_rows
    running = (
        jnp.full((KVH, group_size, tok_rows), neg_fill, jnp.float32),
        jnp.zeros((KVH, group_size, tok_rows), jnp.float32),
        jnp.zeros((tok_rows, KVH, group_size, HD), jnp.float32),
    )
    for block in range(blocks):
        block_start = block * block_rows
        key_block = key_piece[block_start : block_start + block_rows]
        value_block = value_piece[block_start : block_start + block_rows]
        columns = block_start + jnp.arange(block_rows)
        causal = (columns[None, :] <= row_pos[:, None]) & (columns < length)[None, :]
        seg_scores = (
            jnp.einsum("tgjd,ugd->gjtu", queries, key_block, preferred_element_type=jnp.float32)
            * score_scale
        )
        seg_top, seg_total, seg_weights, seg_factor = softmax_step(
            running[0], running[1], seg_scores, causal
        )
        seg_acc = running[2] * jnp.transpose(seg_factor, (2, 0, 1))[..., None] + jnp.einsum(
            "gjtu,ugd->tgjd", seg_weights, value_block, preferred_element_type=jnp.float32
        )
        running = (seg_top, seg_total, seg_acc)

    memory_all = gathered(memory_in.astype(jnp.bfloat16), "tok", ((3, 4), (1, 2), (0,))).reshape(
        -1, 2 * width_kv
    )
    mem_keys = memory_all[:, :width_kv].reshape(-1, KVH, HD)
    mem_vals = memory_all[:, width_kv:].reshape(-1, KVH, HD)
    mem_scores = (
        jnp.einsum("tgjd,mgd->gjtm", queries, mem_keys, preferred_element_type=jnp.float32)
        * score_scale
    )
    row_top = jnp.maximum(running[0], jnp.max(mem_scores, axis=-1))
    seg_factor = jnp.exp(running[0] - row_top)
    mem_weights = jnp.exp(mem_scores - row_top[..., None])
    row_total = running[1] * seg_factor + jnp.sum(mem_weights, axis=-1)
    weighted = running[2] * jnp.transpose(seg_factor, (2, 0, 1))[..., None] + jnp.einsum(
        "gjtm,mgd->tgjd",
        mem_weights.astype(jnp.bfloat16),
        mem_vals,
        preferred_element_type=jnp.float32,
    )
    att_rows = weighted / jnp.transpose(row_total, (2, 0, 1))[..., None]
    log_total = row_top + jnp.log(row_total)
    attended = att_rows.reshape(1, tok_rows, QH * HD).astype(jnp.bfloat16)
    valid_rows = (row_pos < length).astype(jnp.bfloat16)[:, None]
    cotangent = (grad_out[0] * valid_rows * loss_scale).reshape(tok_rows, KVH, group_size, HD)
    row_delta = jnp.einsum("tgjd,tgjd->gjt", cotangent.astype(jnp.float32), att_rows)
    mem_prob = jnp.exp(mem_scores - log_total[..., None])
    grad_prob = jnp.einsum(
        "tgjd,mgd->gjtm", cotangent, mem_vals, preferred_element_type=jnp.float32
    )
    grad_score = mem_prob * (grad_prob - row_delta[..., None])
    grad_vals = jnp.einsum(
        "gjtm,tgjd->mgd",
        mem_prob.astype(jnp.bfloat16),
        cotangent,
        preferred_element_type=jnp.float32,
    )
    grad_keys = (
        jnp.einsum(
            "gjtm,tgjd->mgd",
            grad_score.astype(jnp.bfloat16),
            queries,
            preferred_element_type=jnp.float32,
        )
        * score_scale
    )
    grad_slots = jnp.concatenate(
        [grad_keys.reshape(-1, width_kv), grad_vals.reshape(-1, width_kv)], axis=1
    )
    tok_count = lax.axis_size("tok")
    grad_parts = lax.all_to_all(grad_slots, "tok", 0, 0, tiled=True)
    local_grad = jnp.sum(grad_parts.reshape((tok_count, mem_rows) + grad_parts.shape[1:]), axis=0)

    all_local = gathered(local_grad, "seg", ((2, 3), (0, 1)))
    memory_grad = all_local[seg_count - 1]
    for step in range(seg_count - 2, -1, -1):
        earlier_grad = all_local[step] + all_decay[step] * memory_grad
        memory_grad = jnp.where(step >= seg_index, earlier_grad, memory_grad)
    return (attended, memory_in[None], memory_grad[None])


def solution(mesh):
    placed = (
        P("seg", "tok", None),
        P("seg", "tok", None),
        P("seg", "tok", None),
        P("seg", "tok", None),
        P("tok", None),
        P("tok", None),
        P("seg", None),
        P(),
        P(),
    )
    return jax.shard_map(
        shards,
        mesh=mesh,
        in_specs=placed,
        out_specs=(P("seg", "tok", None), P("seg", "tok", None), P("seg", "tok", None)),
        check_vma=False,
    )
```

```python
import math

import jax
import jax.numpy as jnp
from jax import lax
from jax.sharding import PartitionSpec as P

HD = 128
QH = 16
KVH = 4


loss_scale = 16.0
neg_fill = -1e30
norm_eps = 1e-06


def gathered(block, axis, groups):
    size = lax.axis_size(axis)
    index = lax.axis_index(axis)
    held = block[None]
    axis_bits = []
    for group in groups:
        group = sorted(group)
        mine = sum(((index >> bit) & 1) << k for k, bit in enumerate(group))
        arrived = [held]
        for mask in range(1, 1 << len(group)):
            flip = sum(((mask >> k) & 1) << bit for k, bit in enumerate(group))
            arrived.append(lax.ppermute(held, axis, [(i, i ^ flip) for i in range(size)]))
        placed = []
        for place in range(1 << len(group)):
            value = arrived[0]
            for mask in range(1, 1 << len(group)):
                value = jnp.where((mine ^ mask) == place, arrived[mask], value)
            placed.append(value)
        held = jnp.stack(placed).reshape((2,) * len(group) + held.shape)
        axis_bits = group[::-1] + axis_bits
    order = sorted(range(len(axis_bits)), key=lambda k: -axis_bits[k])
    held = jnp.transpose(held, order + list(range(len(axis_bits), held.ndim)))
    return held.reshape((size,) + block.shape)


def scattered_sum(rows, axis, groups):
    size = lax.axis_size(axis)
    index = lax.axis_index(axis)
    held = rows.reshape((size, rows.shape[0] // size) + rows.shape[1:])
    low = 0
    for width in groups:
        ways = 1 << width
        held = held.reshape((held.shape[0] // ways, ways) + held.shape[1:])
        mine = (index >> low) & (ways - 1)
        total = lax.dynamic_index_in_dim(held, mine, axis=1, keepdims=False)
        for mask in range(1, ways):
            send = lax.dynamic_index_in_dim(held, mine ^ mask, axis=1, keepdims=False)
            flip = mask << low
            total = total + lax.ppermute(send, axis, [(i, i ^ flip) for i in range(size)])
        held = total
        low += width
    return held[0]


def slot_norm(raw_rows):
    parts = raw_rows.reshape(raw_rows.shape[0], 2 * KVH, HD)
    multiplier = lax.rsqrt(jnp.mean(parts * parts, axis=-1, keepdims=True) + norm_eps)
    return (parts * multiplier).reshape(raw_rows.shape)


def softmax_step(row_top, row_total, scores, allowed):
    scores = jnp.where(allowed, scores, neg_fill)
    new_top = jnp.maximum(row_top, jnp.max(scores, axis=-1))
    weights = jnp.where(allowed, jnp.exp(scores - new_top[..., None]), 0.0)
    multiplier = jnp.exp(row_top - new_top)
    new_total = row_total * multiplier + jnp.sum(weights, axis=-1)
    return (new_top, new_total, weights.astype(jnp.bfloat16), multiplier)


def shards(
    seg_queries, seg_keys, seg_values, grad_out, mem_init, mem_query, retention, seg_len, doc_start
):
    tok_rows = seg_queries.shape[1]
    mem_rows = mem_query.shape[0]
    group_size = QH // KVH
    width_kv = KVH * HD
    seg_count = lax.axis_size("seg")
    seg_index = lax.axis_index("seg")
    tok_index = lax.axis_index("tok")
    length = seg_len[seg_index]
    score_scale = 1.0 / math.sqrt(HD)
    queries = seg_queries[0].reshape(tok_rows, KVH, group_size, HD)
    slot_queries = mem_query.reshape(mem_rows, KVH, HD)
    row_pos = tok_index * tok_rows + jnp.arange(tok_rows)

    kv_piece = lax.all_gather(
        jnp.concatenate([seg_keys[0], seg_values[0]], axis=1), "tok", axis=0, tiled=True
    )
    piece_rows = kv_piece.shape[0]
    key_piece = kv_piece[:, :width_kv].reshape(piece_rows, KVH, HD)
    value_piece = kv_piece[:, width_kv:].reshape(piece_rows, KVH, HD)

    live_keys = jnp.arange(piece_rows) < length
    slot_scores = (
        jnp.einsum("rgd,ugd->gru", slot_queries, key_piece, preferred_element_type=jnp.float32)
        * score_scale
    )
    slot_scores = jnp.where(live_keys, slot_scores, neg_fill)
    slot_top = jnp.max(slot_scores, axis=-1, keepdims=True)
    slot_exp = jnp.where(live_keys, jnp.exp(slot_scores - slot_top), 0.0)
    slot_denom = jnp.transpose(jnp.sum(slot_exp, axis=-1))[..., None]
    slot_weights = slot_exp.astype(jnp.bfloat16)
    slot_keys = jnp.einsum(
        "gru,ugd->rgd", slot_weights, key_piece, preferred_element_type=jnp.float32
    )
    slot_values = jnp.einsum(
        "gru,ugd->rgd", slot_weights, value_piece, preferred_element_type=jnp.float32
    )
    raw_slots = jnp.concatenate(
        [
            (slot_keys / slot_denom).reshape(mem_rows, width_kv),
            (slot_values / slot_denom).reshape(mem_rows, width_kv),
        ],
        axis=1,
    )
    written = slot_norm(raw_slots)
    ret_row = retention[0]
    following = doc_start[jnp.minimum(seg_index + 1, seg_count - 1)].astype(jnp.float32)
    keep_flag = jnp.where(seg_index == seg_count - 1, 1.0, 1.0 - following)
    decay_rate = keep_flag * ret_row
    carried = keep_flag * (1.0 - ret_row) * written + (1.0 - keep_flag) * mem_init

    chain_terms = gathered(
        jnp.concatenate([carried, decay_rate[None]], axis=0), "seg", ((2, 3), (0, 1))
    )
    all_carried = chain_terms[:, :mem_rows]
    all_decay = chain_terms[:, mem_rows]
    memory_in = mem_init
    for step in range(seg_count - 1):
        following_memory = all_decay[step] * memory_in + all_carried[step]
        memory_in = jnp.where(step < seg_index, following_memory, memory_in)

    block_rows = math.gcd(piece_rows, 1024)
    blocks = piece_rows // block_rows
    running = (
        jnp.full((KVH, group_size, tok_rows), neg_fill, jnp.float32),
        jnp.zeros((KVH, group_size, tok_rows), jnp.float32),
        jnp.zeros((tok_rows, KVH, group_size, HD), jnp.float32),
    )
    for block in range(blocks):
        block_start = block * block_rows
        key_block = key_piece[block_start : block_start + block_rows]
        value_block = value_piece[block_start : block_start + block_rows]
        columns = block_start + jnp.arange(block_rows)
        causal = (columns[None, :] <= row_pos[:, None]) & (columns < length)[None, :]
        seg_scores = (
            jnp.einsum("tgjd,ugd->gjtu", queries, key_block, preferred_element_type=jnp.float32)
            * score_scale
        )
        seg_top, seg_total, seg_weights, seg_factor = softmax_step(
            running[0], running[1], seg_scores, causal
        )
        seg_acc = running[2] * jnp.transpose(seg_factor, (2, 0, 1))[..., None] + jnp.einsum(
            "gjtu,ugd->tgjd", seg_weights, value_block, preferred_element_type=jnp.float32
        )
        running = (seg_top, seg_total, seg_acc)

    memory_all = gathered(memory_in.astype(jnp.bfloat16), "tok", ((3, 4), (1, 2), (0,))).reshape(
        -1, 2 * width_kv
    )
    mem_keys = memory_all[:, :width_kv].reshape(-1, KVH, HD)
    mem_vals = memory_all[:, width_kv:].reshape(-1, KVH, HD)
    mem_scores = (
        jnp.einsum("tgjd,mgd->gjtm", queries, mem_keys, preferred_element_type=jnp.float32)
        * score_scale
    )
    row_top = jnp.maximum(running[0], jnp.max(mem_scores, axis=-1))
    seg_factor = jnp.exp(running[0] - row_top)
    mem_weights = jnp.exp(mem_scores - row_top[..., None])
    row_total = running[1] * seg_factor + jnp.sum(mem_weights, axis=-1)
    weighted = running[2] * jnp.transpose(seg_factor, (2, 0, 1))[..., None] + jnp.einsum(
        "gjtm,mgd->tgjd",
        mem_weights.astype(jnp.bfloat16),
        mem_vals,
        preferred_element_type=jnp.float32,
    )
    att_rows = weighted / jnp.transpose(row_total, (2, 0, 1))[..., None]
    log_total = row_top + jnp.log(row_total)
    attended = att_rows.reshape(1, tok_rows, QH * HD).astype(jnp.bfloat16)
    valid_rows = (row_pos < length).astype(jnp.bfloat16)[:, None]
    cotangent = (grad_out[0] * valid_rows * loss_scale).reshape(tok_rows, KVH, group_size, HD)
    row_delta = jnp.einsum("tgjd,tgjd->gjt", cotangent.astype(jnp.float32), att_rows)
    mem_prob = jnp.exp(mem_scores - log_total[..., None])
    grad_prob = jnp.einsum(
        "tgjd,mgd->gjtm", cotangent, mem_vals, preferred_element_type=jnp.float32
    )
    grad_score = mem_prob * (grad_prob - row_delta[..., None])
    grad_vals = jnp.einsum(
        "gjtm,tgjd->mgd",
        mem_prob.astype(jnp.bfloat16),
        cotangent,
        preferred_element_type=jnp.float32,
    )
    grad_keys = (
        jnp.einsum(
            "gjtm,tgjd->mgd",
            grad_score.astype(jnp.bfloat16),
            queries,
            preferred_element_type=jnp.float32,
        )
        * score_scale
    )
    grad_slots = jnp.concatenate(
        [grad_keys.reshape(-1, width_kv), grad_vals.reshape(-1, width_kv)], axis=1
    )
    local_grad = scattered_sum(grad_slots, "tok", (1, 2, 2))

    all_local = gathered(local_grad, "seg", ((2, 3), (0, 1)))
    memory_grad = all_local[seg_count - 1]
    for step in range(seg_count - 2, -1, -1):
        earlier_grad = all_local[step] + all_decay[step] * memory_grad
        memory_grad = jnp.where(step >= seg_index, earlier_grad, memory_grad)
    return (attended, memory_in[None], memory_grad[None])


def solution(mesh):
    placed = (
        P("seg", "tok", None),
        P("seg", "tok", None),
        P("seg", "tok", None),
        P("seg", "tok", None),
        P("tok", None),
        P("tok", None),
        P("seg", None),
        P(),
        P(),
    )
    return jax.shard_map(
        shards,
        mesh=mesh,
        in_specs=placed,
        out_specs=(P("seg", "tok", None), P("seg", "tok", None), P("seg", "tok", None)),
        check_vma=False,
    )
```

```python
import math

import jax
import jax.numpy as jnp
from jax import lax
from jax.sharding import PartitionSpec as P

HD = 128
QH = 16
KVH = 4


loss_scale = 16.0
neg_fill = -1e30
norm_eps = 1e-06


def gathered(block, axis, groups):
    size = lax.axis_size(axis)
    index = lax.axis_index(axis)
    held = block[None]
    axis_bits = []
    for group in groups:
        group = sorted(group)
        mine = sum(((index >> bit) & 1) << k for k, bit in enumerate(group))
        arrived = [held]
        for mask in range(1, 1 << len(group)):
            flip = sum(((mask >> k) & 1) << bit for k, bit in enumerate(group))
            arrived.append(lax.ppermute(held, axis, [(i, i ^ flip) for i in range(size)]))
        placed = []
        for place in range(1 << len(group)):
            value = arrived[0]
            for mask in range(1, 1 << len(group)):
                value = jnp.where((mine ^ mask) == place, arrived[mask], value)
            placed.append(value)
        held = jnp.stack(placed).reshape((2,) * len(group) + held.shape)
        axis_bits = group[::-1] + axis_bits
    order = sorted(range(len(axis_bits)), key=lambda k: -axis_bits[k])
    held = jnp.transpose(held, order + list(range(len(axis_bits), held.ndim)))
    return held.reshape((size,) + block.shape)


def scattered_sum(rows, axis, groups):
    size = lax.axis_size(axis)
    index = lax.axis_index(axis)
    held = rows.reshape((size, rows.shape[0] // size) + rows.shape[1:])
    low = 0
    for width in groups:
        ways = 1 << width
        held = held.reshape((held.shape[0] // ways, ways) + held.shape[1:])
        mine = (index >> low) & (ways - 1)
        total = lax.dynamic_index_in_dim(held, mine, axis=1, keepdims=False)
        for mask in range(1, ways):
            send = lax.dynamic_index_in_dim(held, mine ^ mask, axis=1, keepdims=False)
            flip = mask << low
            total = total + lax.ppermute(send, axis, [(i, i ^ flip) for i in range(size)])
        held = total
        low += width
    return held[0]


def slot_norm(raw_rows):
    parts = raw_rows.reshape(raw_rows.shape[0], 2 * KVH, HD)
    multiplier = lax.rsqrt(jnp.mean(parts * parts, axis=-1, keepdims=True) + norm_eps)
    return (parts * multiplier).reshape(raw_rows.shape)


def softmax_step(row_top, row_total, scores, allowed):
    scores = jnp.where(allowed, scores, neg_fill)
    new_top = jnp.maximum(row_top, jnp.max(scores, axis=-1))
    weights = jnp.where(allowed, jnp.exp(scores - new_top[..., None]), 0.0)
    multiplier = jnp.exp(row_top - new_top)
    new_total = row_total * multiplier + jnp.sum(weights, axis=-1)
    return (new_top, new_total, weights.astype(jnp.bfloat16), multiplier)


def shards(
    seg_queries, seg_keys, seg_values, grad_out, mem_init, mem_query, retention, seg_len, doc_start
):
    tok_rows = seg_queries.shape[1]
    mem_rows = mem_query.shape[0]
    group_size = QH // KVH
    width_kv = KVH * HD
    seg_count = lax.axis_size("seg")
    seg_index = lax.axis_index("seg")
    tok_index = lax.axis_index("tok")
    length = seg_len[seg_index]
    score_scale = 1.0 / math.sqrt(HD)
    queries = seg_queries[0].reshape(tok_rows, KVH, group_size, HD)
    slot_queries = mem_query.reshape(mem_rows, KVH, HD)
    row_pos = tok_index * tok_rows + jnp.arange(tok_rows)

    kv_piece = lax.all_gather(
        jnp.concatenate([seg_keys[0], seg_values[0]], axis=1), "tok", axis=0, tiled=True
    )
    piece_rows = kv_piece.shape[0]
    key_piece = kv_piece[:, :width_kv].reshape(piece_rows, KVH, HD)
    value_piece = kv_piece[:, width_kv:].reshape(piece_rows, KVH, HD)

    live_keys = jnp.arange(piece_rows) < length
    slot_scores = (
        jnp.einsum("rgd,ugd->gru", slot_queries, key_piece, preferred_element_type=jnp.float32)
        * score_scale
    )
    slot_scores = jnp.where(live_keys, slot_scores, neg_fill)
    slot_top = jnp.max(slot_scores, axis=-1, keepdims=True)
    slot_exp = jnp.where(live_keys, jnp.exp(slot_scores - slot_top), 0.0)
    slot_denom = jnp.transpose(jnp.sum(slot_exp, axis=-1))[..., None]
    slot_weights = slot_exp.astype(jnp.bfloat16)
    slot_keys = jnp.einsum(
        "gru,ugd->rgd", slot_weights, key_piece, preferred_element_type=jnp.float32
    )
    slot_values = jnp.einsum(
        "gru,ugd->rgd", slot_weights, value_piece, preferred_element_type=jnp.float32
    )
    raw_slots = jnp.concatenate(
        [
            (slot_keys / slot_denom).reshape(mem_rows, width_kv),
            (slot_values / slot_denom).reshape(mem_rows, width_kv),
        ],
        axis=1,
    )
    written = slot_norm(raw_slots)
    ret_row = retention[0]
    following = doc_start[jnp.minimum(seg_index + 1, seg_count - 1)].astype(jnp.float32)
    keep_flag = jnp.where(seg_index == seg_count - 1, 1.0, 1.0 - following)
    decay_rate = keep_flag * ret_row
    carried = keep_flag * (1.0 - ret_row) * written + (1.0 - keep_flag) * mem_init

    chain_terms = gathered(
        jnp.concatenate([carried, decay_rate[None]], axis=0), "seg", ((2, 3), (0, 1))
    )
    all_carried = chain_terms[:, :mem_rows]
    all_decay = chain_terms[:, mem_rows]
    memory_in = mem_init
    for step in range(seg_count - 1):
        following_memory = all_decay[step] * memory_in + all_carried[step]
        memory_in = jnp.where(step < seg_index, following_memory, memory_in)

    block_rows = math.gcd(piece_rows, 2048)
    blocks = piece_rows // block_rows
    running = (
        jnp.full((KVH, group_size, tok_rows), neg_fill, jnp.float32),
        jnp.zeros((KVH, group_size, tok_rows), jnp.float32),
        jnp.zeros((tok_rows, KVH, group_size, HD), jnp.float32),
    )
    for block in range(blocks):
        block_start = block * block_rows
        key_block = key_piece[block_start : block_start + block_rows]
        value_block = value_piece[block_start : block_start + block_rows]
        columns = block_start + jnp.arange(block_rows)
        causal = (columns[None, :] <= row_pos[:, None]) & (columns < length)[None, :]
        seg_scores = (
            jnp.einsum("tgjd,ugd->gjtu", queries, key_block, preferred_element_type=jnp.float32)
            * score_scale
        )
        seg_top, seg_total, seg_weights, seg_factor = softmax_step(
            running[0], running[1], seg_scores, causal
        )
        seg_acc = running[2] * jnp.transpose(seg_factor, (2, 0, 1))[..., None] + jnp.einsum(
            "gjtu,ugd->tgjd", seg_weights, value_block, preferred_element_type=jnp.float32
        )
        running = (seg_top, seg_total, seg_acc)

    memory_all = gathered(memory_in.astype(jnp.bfloat16), "tok", ((3, 4), (1, 2), (0,))).reshape(
        -1, 2 * width_kv
    )
    mem_keys = memory_all[:, :width_kv].reshape(-1, KVH, HD)
    mem_vals = memory_all[:, width_kv:].reshape(-1, KVH, HD)
    mem_scores = (
        jnp.einsum("tgjd,mgd->gjtm", queries, mem_keys, preferred_element_type=jnp.float32)
        * score_scale
    )
    row_top = jnp.maximum(running[0], jnp.max(mem_scores, axis=-1))
    seg_factor = jnp.exp(running[0] - row_top)
    mem_weights = jnp.exp(mem_scores - row_top[..., None])
    row_total = running[1] * seg_factor + jnp.sum(mem_weights, axis=-1)
    weighted = running[2] * jnp.transpose(seg_factor, (2, 0, 1))[..., None] + jnp.einsum(
        "gjtm,mgd->tgjd",
        mem_weights.astype(jnp.bfloat16),
        mem_vals,
        preferred_element_type=jnp.float32,
    )
    att_rows = weighted / jnp.transpose(row_total, (2, 0, 1))[..., None]
    log_total = row_top + jnp.log(row_total)
    attended = att_rows.reshape(1, tok_rows, QH * HD).astype(jnp.bfloat16)
    valid_rows = (row_pos < length).astype(jnp.bfloat16)[:, None]
    cotangent = (grad_out[0] * valid_rows * loss_scale).reshape(tok_rows, KVH, group_size, HD)
    row_delta = jnp.einsum("tgjd,tgjd->gjt", cotangent.astype(jnp.float32), att_rows)
    mem_prob = jnp.exp(mem_scores - log_total[..., None])
    grad_prob = jnp.einsum(
        "tgjd,mgd->gjtm", cotangent, mem_vals, preferred_element_type=jnp.float32
    )
    grad_score = mem_prob * (grad_prob - row_delta[..., None])
    grad_vals = jnp.einsum(
        "gjtm,tgjd->mgd",
        mem_prob.astype(jnp.bfloat16),
        cotangent,
        preferred_element_type=jnp.float32,
    )
    grad_keys = (
        jnp.einsum(
            "gjtm,tgjd->mgd",
            grad_score.astype(jnp.bfloat16),
            queries,
            preferred_element_type=jnp.float32,
        )
        * score_scale
    )
    grad_slots = jnp.concatenate(
        [grad_keys.reshape(-1, width_kv), grad_vals.reshape(-1, width_kv)], axis=1
    )
    local_grad = scattered_sum(grad_slots, "tok", (1, 2, 2))

    all_local = gathered(local_grad, "seg", ((2, 3), (0, 1)))
    memory_grad = all_local[seg_count - 1]
    for step in range(seg_count - 2, -1, -1):
        earlier_grad = all_local[step] + all_decay[step] * memory_grad
        memory_grad = jnp.where(step >= seg_index, earlier_grad, memory_grad)
    return (attended, memory_in[None], memory_grad[None])


def solution(mesh):
    placed = (
        P("seg", "tok", None),
        P("seg", "tok", None),
        P("seg", "tok", None),
        P("seg", "tok", None),
        P("tok", None),
        P("tok", None),
        P("seg", None),
        P(),
        P(),
    )
    return jax.shard_map(
        shards,
        mesh=mesh,
        in_specs=placed,
        out_specs=(P("seg", "tok", None), P("seg", "tok", None), P("seg", "tok", None)),
        check_vma=False,
    )
```

```python
import math

import jax
import jax.numpy as jnp
from jax import lax
from jax.sharding import PartitionSpec as P

HD = 128
QH = 16
KVH = 4


loss_scale = 16.0
neg_fill = -1e30
norm_eps = 1e-06


def gathered(block, axis, groups):
    size = lax.axis_size(axis)
    index = lax.axis_index(axis)
    held = block[None]
    axis_bits = []
    for group in groups:
        group = sorted(group)
        mine = sum(((index >> bit) & 1) << k for k, bit in enumerate(group))
        arrived = [held]
        for mask in range(1, 1 << len(group)):
            flip = sum(((mask >> k) & 1) << bit for k, bit in enumerate(group))
            arrived.append(lax.ppermute(held, axis, [(i, i ^ flip) for i in range(size)]))
        placed = []
        for place in range(1 << len(group)):
            value = arrived[0]
            for mask in range(1, 1 << len(group)):
                value = jnp.where((mine ^ mask) == place, arrived[mask], value)
            placed.append(value)
        held = jnp.stack(placed).reshape((2,) * len(group) + held.shape)
        axis_bits = group[::-1] + axis_bits
    order = sorted(range(len(axis_bits)), key=lambda k: -axis_bits[k])
    held = jnp.transpose(held, order + list(range(len(axis_bits), held.ndim)))
    return held.reshape((size,) + block.shape)


def scattered_sum(rows, axis, groups):
    size = lax.axis_size(axis)
    index = lax.axis_index(axis)
    held = rows.reshape((size, rows.shape[0] // size) + rows.shape[1:])
    low = 0
    for width in groups:
        ways = 1 << width
        held = held.reshape((held.shape[0] // ways, ways) + held.shape[1:])
        mine = (index >> low) & (ways - 1)
        total = lax.dynamic_index_in_dim(held, mine, axis=1, keepdims=False)
        for mask in range(1, ways):
            send = lax.dynamic_index_in_dim(held, mine ^ mask, axis=1, keepdims=False)
            flip = mask << low
            total = total + lax.ppermute(send, axis, [(i, i ^ flip) for i in range(size)])
        held = total
        low += width
    return held[0]


def slot_norm(raw_rows):
    parts = raw_rows.reshape(raw_rows.shape[0], 2 * KVH, HD)
    multiplier = lax.rsqrt(jnp.mean(parts * parts, axis=-1, keepdims=True) + norm_eps)
    return (parts * multiplier).reshape(raw_rows.shape)


def softmax_step(row_top, row_total, scores, allowed):
    scores = jnp.where(allowed, scores, neg_fill)
    new_top = jnp.maximum(row_top, jnp.max(scores, axis=-1))
    weights = jnp.where(allowed, jnp.exp(scores - new_top[..., None]), 0.0)
    multiplier = jnp.exp(row_top - new_top)
    new_total = row_total * multiplier + jnp.sum(weights, axis=-1)
    return (new_top, new_total, weights.astype(jnp.bfloat16), multiplier)


def shards(
    seg_queries, seg_keys, seg_values, grad_out, mem_init, mem_query, retention, seg_len, doc_start
):
    tok_rows = seg_queries.shape[1]
    mem_rows = mem_query.shape[0]
    group_size = QH // KVH
    width_kv = KVH * HD
    seg_count = lax.axis_size("seg")
    seg_index = lax.axis_index("seg")
    tok_index = lax.axis_index("tok")
    length = seg_len[seg_index]
    score_scale = 1.0 / math.sqrt(HD)
    queries = seg_queries[0].reshape(tok_rows, KVH, group_size, HD)
    slot_queries = mem_query.reshape(mem_rows, KVH, HD)
    row_pos = tok_index * tok_rows + jnp.arange(tok_rows)

    kv_piece = lax.all_gather(
        jnp.concatenate([seg_keys[0], seg_values[0]], axis=1), "tok", axis=0, tiled=True
    )
    piece_rows = kv_piece.shape[0]
    key_piece = kv_piece[:, :width_kv].reshape(piece_rows, KVH, HD)
    value_piece = kv_piece[:, width_kv:].reshape(piece_rows, KVH, HD)

    live_keys = jnp.arange(piece_rows) < length
    slot_scores = (
        jnp.einsum("rgd,ugd->gru", slot_queries, key_piece, preferred_element_type=jnp.float32)
        * score_scale
    )
    slot_scores = jnp.where(live_keys, slot_scores, neg_fill)
    slot_top = jnp.max(slot_scores, axis=-1, keepdims=True)
    slot_exp = jnp.where(live_keys, jnp.exp(slot_scores - slot_top), 0.0)
    slot_denom = jnp.transpose(jnp.sum(slot_exp, axis=-1))[..., None]
    slot_weights = slot_exp.astype(jnp.bfloat16)
    slot_keys = jnp.einsum(
        "gru,ugd->rgd", slot_weights, key_piece, preferred_element_type=jnp.float32
    )
    slot_values = jnp.einsum(
        "gru,ugd->rgd", slot_weights, value_piece, preferred_element_type=jnp.float32
    )
    raw_slots = jnp.concatenate(
        [
            (slot_keys / slot_denom).reshape(mem_rows, width_kv),
            (slot_values / slot_denom).reshape(mem_rows, width_kv),
        ],
        axis=1,
    )
    written = slot_norm(raw_slots)
    ret_row = retention[0]
    following = doc_start[jnp.minimum(seg_index + 1, seg_count - 1)].astype(jnp.float32)
    keep_flag = jnp.where(seg_index == seg_count - 1, 1.0, 1.0 - following)
    decay_rate = keep_flag * ret_row
    carried = keep_flag * (1.0 - ret_row) * written + (1.0 - keep_flag) * mem_init

    chain_terms = gathered(
        jnp.concatenate([carried, decay_rate[None]], axis=0), "seg", ((2, 3), (0, 1))
    )
    all_carried = chain_terms[:, :mem_rows]
    all_decay = chain_terms[:, mem_rows]
    memory_in = mem_init
    for step in range(seg_count - 1):
        following_memory = all_decay[step] * memory_in + all_carried[step]
        memory_in = jnp.where(step < seg_index, following_memory, memory_in)

    block_rows = math.gcd(piece_rows, 1024)
    blocks = piece_rows // block_rows
    running = (
        jnp.full((KVH, group_size, tok_rows), neg_fill, jnp.float32),
        jnp.zeros((KVH, group_size, tok_rows), jnp.float32),
        jnp.zeros((tok_rows, KVH, group_size, HD), jnp.float32),
    )
    for block in range(blocks):
        block_start = block * block_rows
        key_block = key_piece[block_start : block_start + block_rows]
        value_block = value_piece[block_start : block_start + block_rows]
        columns = block_start + jnp.arange(block_rows)
        causal = (columns[None, :] <= row_pos[:, None]) & (columns < length)[None, :]
        seg_scores = (
            jnp.einsum("tgjd,ugd->gjtu", queries, key_block, preferred_element_type=jnp.float32)
            * score_scale
        )
        seg_top, seg_total, seg_weights, seg_factor = softmax_step(
            running[0], running[1], seg_scores, causal
        )
        seg_acc = running[2] * jnp.transpose(seg_factor, (2, 0, 1))[..., None] + jnp.einsum(
            "gjtu,ugd->tgjd", seg_weights, value_block, preferred_element_type=jnp.float32
        )
        running = (seg_top, seg_total, seg_acc)

    memory_all = gathered(memory_in.astype(jnp.bfloat16), "tok", ((3, 4), (1, 2), (0,))).reshape(
        -1, 2 * width_kv
    )
    mem_keys = memory_all[:, :width_kv].reshape(-1, KVH, HD)
    mem_vals = memory_all[:, width_kv:].reshape(-1, KVH, HD)
    mem_scores = (
        jnp.einsum("tgjd,mgd->gjtm", queries, mem_keys, preferred_element_type=jnp.float32)
        * score_scale
    )
    row_top = jnp.maximum(running[0], jnp.max(mem_scores, axis=-1))
    seg_factor = jnp.exp(running[0] - row_top)
    mem_weights = jnp.exp(mem_scores - row_top[..., None])
    row_total = running[1] * seg_factor + jnp.sum(mem_weights, axis=-1)
    weighted = running[2] * jnp.transpose(seg_factor, (2, 0, 1))[..., None] + jnp.einsum(
        "gjtm,mgd->tgjd",
        mem_weights.astype(jnp.bfloat16),
        mem_vals,
        preferred_element_type=jnp.float32,
    )
    att_rows = weighted / jnp.transpose(row_total, (2, 0, 1))[..., None]
    log_total = row_top + jnp.log(row_total)
    attended = att_rows.reshape(1, tok_rows, QH * HD).astype(jnp.bfloat16)
    valid_rows = (row_pos < length).astype(jnp.bfloat16)[:, None]
    cotangent = (grad_out[0] * valid_rows * loss_scale).reshape(tok_rows, KVH, group_size, HD)
    row_delta = jnp.einsum("tgjd,tgjd->gjt", cotangent.astype(jnp.float32), att_rows)
    mem_prob = jnp.exp(mem_scores - log_total[..., None])
    grad_prob = jnp.einsum(
        "tgjd,mgd->gjtm", cotangent, mem_vals, preferred_element_type=jnp.float32
    )
    grad_score = mem_prob * (grad_prob - row_delta[..., None])
    grad_vals = jnp.einsum(
        "gjtm,tgjd->mgd",
        mem_prob.astype(jnp.bfloat16),
        cotangent,
        preferred_element_type=jnp.float32,
    )
    grad_keys = (
        jnp.einsum(
            "gjtm,tgjd->mgd",
            grad_score.astype(jnp.bfloat16),
            queries,
            preferred_element_type=jnp.float32,
        )
        * score_scale
    )
    grad_slots = jnp.concatenate(
        [grad_keys.reshape(-1, width_kv), grad_vals.reshape(-1, width_kv)], axis=1
    )
    local_grad = scattered_sum(grad_slots, "tok", (1, 2, 2))

    grad_terms = jnp.concatenate([local_grad, decay_rate[None]], axis=0)
    distance = 1
    while distance < seg_count:
        route = [(i, i - distance) for i in range(distance, seg_count)]
        arrived = lax.ppermute(grad_terms, "seg", route)
        own_decay = grad_terms[mem_rows]
        grad_terms = jnp.concatenate(
            [
                grad_terms[:mem_rows] + own_decay * arrived[:mem_rows],
                (own_decay * arrived[mem_rows])[None],
            ],
            axis=0,
        )
        distance *= 2
    memory_grad = grad_terms[:mem_rows]
    return (attended, memory_in[None], memory_grad[None])


def solution(mesh):
    placed = (
        P("seg", "tok", None),
        P("seg", "tok", None),
        P("seg", "tok", None),
        P("seg", "tok", None),
        P("tok", None),
        P("tok", None),
        P("seg", None),
        P(),
        P(),
    )
    return jax.shard_map(
        shards,
        mesh=mesh,
        in_specs=placed,
        out_specs=(P("seg", "tok", None), P("seg", "tok", None), P("seg", "tok", None)),
        check_vma=False,
    )
```

```python
import math

import jax
import jax.numpy as jnp
from jax import lax
from jax.sharding import PartitionSpec as P

HD = 128
QH = 16
KVH = 4


loss_scale = 16.0
neg_fill = -1e30
norm_eps = 1e-06


def gathered(block, axis, groups):
    size = lax.axis_size(axis)
    index = lax.axis_index(axis)
    held = block[None]
    axis_bits = []
    for group in groups:
        group = sorted(group)
        mine = sum(((index >> bit) & 1) << k for k, bit in enumerate(group))
        arrived = [held]
        for mask in range(1, 1 << len(group)):
            flip = sum(((mask >> k) & 1) << bit for k, bit in enumerate(group))
            arrived.append(lax.ppermute(held, axis, [(i, i ^ flip) for i in range(size)]))
        placed = []
        for place in range(1 << len(group)):
            value = arrived[0]
            for mask in range(1, 1 << len(group)):
                value = jnp.where((mine ^ mask) == place, arrived[mask], value)
            placed.append(value)
        held = jnp.stack(placed).reshape((2,) * len(group) + held.shape)
        axis_bits = group[::-1] + axis_bits
    order = sorted(range(len(axis_bits)), key=lambda k: -axis_bits[k])
    held = jnp.transpose(held, order + list(range(len(axis_bits), held.ndim)))
    return held.reshape((size,) + block.shape)


def scattered_sum(rows, axis, groups):
    size = lax.axis_size(axis)
    index = lax.axis_index(axis)
    held = rows.reshape((size, rows.shape[0] // size) + rows.shape[1:])
    low = 0
    for width in groups:
        ways = 1 << width
        held = held.reshape((held.shape[0] // ways, ways) + held.shape[1:])
        mine = (index >> low) & (ways - 1)
        total = lax.dynamic_index_in_dim(held, mine, axis=1, keepdims=False)
        for mask in range(1, ways):
            send = lax.dynamic_index_in_dim(held, mine ^ mask, axis=1, keepdims=False)
            flip = mask << low
            total = total + lax.ppermute(send, axis, [(i, i ^ flip) for i in range(size)])
        held = total
        low += width
    return held[0]


def slot_norm(raw_rows):
    parts = raw_rows.reshape(raw_rows.shape[0], 2 * KVH, HD)
    multiplier = lax.rsqrt(jnp.mean(parts * parts, axis=-1, keepdims=True) + norm_eps)
    return (parts * multiplier).reshape(raw_rows.shape)


def softmax_step(row_top, row_total, scores, allowed):
    scores = jnp.where(allowed, scores, neg_fill)
    new_top = jnp.maximum(row_top, jnp.max(scores, axis=-1))
    weights = jnp.where(allowed, jnp.exp(scores - new_top[..., None]), 0.0)
    multiplier = jnp.exp(row_top - new_top)
    new_total = row_total * multiplier + jnp.sum(weights, axis=-1)
    return (new_top, new_total, weights.astype(jnp.bfloat16), multiplier)


def shards(
    seg_queries, seg_keys, seg_values, grad_out, mem_init, mem_query, retention, seg_len, doc_start
):
    tok_rows = seg_queries.shape[1]
    mem_rows = mem_query.shape[0]
    group_size = QH // KVH
    width_kv = KVH * HD
    seg_count = lax.axis_size("seg")
    seg_index = lax.axis_index("seg")
    tok_index = lax.axis_index("tok")
    length = seg_len[seg_index]
    score_scale = 1.0 / math.sqrt(HD)
    queries = seg_queries[0].reshape(tok_rows, KVH, group_size, HD)
    slot_queries = mem_query.reshape(mem_rows, KVH, HD)
    row_pos = tok_index * tok_rows + jnp.arange(tok_rows)

    kv_piece = lax.all_gather(
        jnp.concatenate([seg_keys[0], seg_values[0]], axis=1), "tok", axis=0, tiled=True
    )
    piece_rows = kv_piece.shape[0]
    key_piece = kv_piece[:, :width_kv].reshape(piece_rows, KVH, HD)
    value_piece = kv_piece[:, width_kv:].reshape(piece_rows, KVH, HD)

    live_keys = jnp.arange(piece_rows) < length
    slot_scores = (
        jnp.einsum("rgd,ugd->gru", slot_queries, key_piece, preferred_element_type=jnp.float32)
        * score_scale
    )
    slot_scores = jnp.where(live_keys, slot_scores, neg_fill)
    slot_top = jnp.max(slot_scores, axis=-1, keepdims=True)
    slot_exp = jnp.where(live_keys, jnp.exp(slot_scores - slot_top), 0.0)
    slot_denom = jnp.transpose(jnp.sum(slot_exp, axis=-1))[..., None]
    slot_weights = slot_exp.astype(jnp.bfloat16)
    slot_keys = jnp.einsum(
        "gru,ugd->rgd", slot_weights, key_piece, preferred_element_type=jnp.float32
    )
    slot_values = jnp.einsum(
        "gru,ugd->rgd", slot_weights, value_piece, preferred_element_type=jnp.float32
    )
    raw_slots = jnp.concatenate(
        [
            (slot_keys / slot_denom).reshape(mem_rows, width_kv),
            (slot_values / slot_denom).reshape(mem_rows, width_kv),
        ],
        axis=1,
    )
    written = slot_norm(raw_slots)
    ret_row = retention[0]
    following = doc_start[jnp.minimum(seg_index + 1, seg_count - 1)].astype(jnp.float32)
    keep_flag = jnp.where(seg_index == seg_count - 1, 1.0, 1.0 - following)
    decay_rate = keep_flag * ret_row
    carried = keep_flag * (1.0 - ret_row) * written + (1.0 - keep_flag) * mem_init

    chain_terms = gathered(
        jnp.concatenate([carried, decay_rate[None]], axis=0), "seg", ((2, 3), (0, 1))
    )
    all_carried = chain_terms[:, :mem_rows]
    all_decay = chain_terms[:, mem_rows]
    memory_in = mem_init
    for step in range(seg_count - 1):
        following_memory = all_decay[step] * memory_in + all_carried[step]
        memory_in = jnp.where(step < seg_index, following_memory, memory_in)

    block_rows = math.gcd(piece_rows, 1024)
    blocks = piece_rows // block_rows
    running = (
        jnp.full((KVH, group_size, tok_rows), neg_fill, jnp.float32),
        jnp.zeros((KVH, group_size, tok_rows), jnp.float32),
        jnp.zeros((tok_rows, KVH, group_size, HD), jnp.float32),
    )
    for block in range(blocks):
        block_start = block * block_rows
        key_block = key_piece[block_start : block_start + block_rows]
        value_block = value_piece[block_start : block_start + block_rows]
        columns = block_start + jnp.arange(block_rows)
        causal = (columns[None, :] <= row_pos[:, None]) & (columns < length)[None, :]
        seg_scores = (
            jnp.einsum("tgjd,ugd->gjtu", queries, key_block, preferred_element_type=jnp.float32)
            * score_scale
        )
        seg_top, seg_total, seg_weights, seg_factor = softmax_step(
            running[0], running[1], seg_scores, causal
        )
        seg_acc = running[2] * jnp.transpose(seg_factor, (2, 0, 1))[..., None] + jnp.einsum(
            "gjtu,ugd->tgjd", seg_weights, value_block, preferred_element_type=jnp.float32
        )
        running = (seg_top, seg_total, seg_acc)

    memory_all = gathered(memory_in.astype(jnp.bfloat16), "tok", ((3, 4), (1, 2), (0,))).reshape(
        -1, 2 * width_kv
    )
    mem_keys = memory_all[:, :width_kv].reshape(-1, KVH, HD)
    mem_vals = memory_all[:, width_kv:].reshape(-1, KVH, HD)
    mem_scores = (
        jnp.einsum("tgjd,mgd->gjtm", queries, mem_keys, preferred_element_type=jnp.float32)
        * score_scale
    )
    row_top = jnp.maximum(running[0], jnp.max(mem_scores, axis=-1))
    seg_factor = jnp.exp(running[0] - row_top)
    mem_weights = jnp.exp(mem_scores - row_top[..., None])
    row_total = running[1] * seg_factor + jnp.sum(mem_weights, axis=-1)
    weighted = running[2] * jnp.transpose(seg_factor, (2, 0, 1))[..., None] + jnp.einsum(
        "gjtm,mgd->tgjd",
        mem_weights.astype(jnp.bfloat16),
        mem_vals,
        preferred_element_type=jnp.float32,
    )
    att_rows = weighted / jnp.transpose(row_total, (2, 0, 1))[..., None]
    log_total = row_top + jnp.log(row_total)
    attended = att_rows.reshape(1, tok_rows, QH * HD).astype(jnp.bfloat16)
    valid_rows = (row_pos < length).astype(jnp.bfloat16)[:, None]
    cotangent = (grad_out[0] * valid_rows * loss_scale).reshape(tok_rows, KVH, group_size, HD)
    row_delta = jnp.einsum("tgjd,tgjd->gjt", cotangent.astype(jnp.float32), att_rows)
    mem_prob = jnp.exp(mem_scores - log_total[..., None])
    grad_prob = jnp.einsum(
        "tgjd,mgd->gjtm", cotangent, mem_vals, preferred_element_type=jnp.float32
    )
    grad_score = mem_prob * (grad_prob - row_delta[..., None])
    grad_vals = jnp.einsum(
        "gjtm,tgjd->mgd",
        mem_prob.astype(jnp.bfloat16),
        cotangent,
        preferred_element_type=jnp.float32,
    )
    grad_keys = (
        jnp.einsum(
            "gjtm,tgjd->mgd",
            grad_score.astype(jnp.bfloat16),
            queries,
            preferred_element_type=jnp.float32,
        )
        * score_scale
    )
    grad_slots = jnp.concatenate(
        [grad_keys.reshape(-1, width_kv), grad_vals.reshape(-1, width_kv)], axis=1
    )
    local_grad = scattered_sum(grad_slots, "tok", (1, 1, 1, 1, 1))

    all_local = gathered(local_grad, "seg", ((2, 3), (0, 1)))
    memory_grad = all_local[seg_count - 1]
    for step in range(seg_count - 2, -1, -1):
        earlier_grad = all_local[step] + all_decay[step] * memory_grad
        memory_grad = jnp.where(step >= seg_index, earlier_grad, memory_grad)
    return (attended, memory_in[None], memory_grad[None])


def solution(mesh):
    placed = (
        P("seg", "tok", None),
        P("seg", "tok", None),
        P("seg", "tok", None),
        P("seg", "tok", None),
        P("tok", None),
        P("tok", None),
        P("seg", None),
        P(),
        P(),
    )
    return jax.shard_map(
        shards,
        mesh=mesh,
        in_specs=placed,
        out_specs=(P("seg", "tok", None), P("seg", "tok", None), P("seg", "tok", None)),
        check_vma=False,
    )
```

```python
import math

import jax
import jax.numpy as jnp
from jax import lax
from jax.sharding import PartitionSpec as P

HD = 128
QH = 16
KVH = 4


loss_scale = 16.0
neg_fill = -1e30
norm_eps = 1e-06


def gathered(block, axis, groups):
    size = lax.axis_size(axis)
    index = lax.axis_index(axis)
    held = block[None]
    axis_bits = []
    for group in groups:
        group = sorted(group)
        mine = sum(((index >> bit) & 1) << k for k, bit in enumerate(group))
        arrived = [held]
        for mask in range(1, 1 << len(group)):
            flip = sum(((mask >> k) & 1) << bit for k, bit in enumerate(group))
            arrived.append(lax.ppermute(held, axis, [(i, i ^ flip) for i in range(size)]))
        placed = []
        for place in range(1 << len(group)):
            value = arrived[0]
            for mask in range(1, 1 << len(group)):
                value = jnp.where((mine ^ mask) == place, arrived[mask], value)
            placed.append(value)
        held = jnp.stack(placed).reshape((2,) * len(group) + held.shape)
        axis_bits = group[::-1] + axis_bits
    order = sorted(range(len(axis_bits)), key=lambda k: -axis_bits[k])
    held = jnp.transpose(held, order + list(range(len(axis_bits), held.ndim)))
    return held.reshape((size,) + block.shape)


def scattered_sum(rows, axis, groups):
    size = lax.axis_size(axis)
    index = lax.axis_index(axis)
    held = rows.reshape((size, rows.shape[0] // size) + rows.shape[1:])
    low = 0
    for width in groups:
        ways = 1 << width
        held = held.reshape((held.shape[0] // ways, ways) + held.shape[1:])
        mine = (index >> low) & (ways - 1)
        total = lax.dynamic_index_in_dim(held, mine, axis=1, keepdims=False)
        for mask in range(1, ways):
            send = lax.dynamic_index_in_dim(held, mine ^ mask, axis=1, keepdims=False)
            flip = mask << low
            total = total + lax.ppermute(send, axis, [(i, i ^ flip) for i in range(size)])
        held = total
        low += width
    return held[0]


def slot_norm(raw_rows):
    parts = raw_rows.reshape(raw_rows.shape[0], 2 * KVH, HD)
    multiplier = lax.rsqrt(jnp.mean(parts * parts, axis=-1, keepdims=True) + norm_eps)
    return (parts * multiplier).reshape(raw_rows.shape)


def softmax_step(row_top, row_total, scores, allowed):
    scores = jnp.where(allowed, scores, neg_fill)
    new_top = jnp.maximum(row_top, jnp.max(scores, axis=-1))
    weights = jnp.where(allowed, jnp.exp(scores - new_top[..., None]), 0.0)
    multiplier = jnp.exp(row_top - new_top)
    new_total = row_total * multiplier + jnp.sum(weights, axis=-1)
    return (new_top, new_total, weights.astype(jnp.bfloat16), multiplier)


def shards(
    seg_queries, seg_keys, seg_values, grad_out, mem_init, mem_query, retention, seg_len, doc_start
):
    tok_rows = seg_queries.shape[1]
    mem_rows = mem_query.shape[0]
    group_size = QH // KVH
    width_kv = KVH * HD
    seg_count = lax.axis_size("seg")
    seg_index = lax.axis_index("seg")
    tok_index = lax.axis_index("tok")
    length = seg_len[seg_index]
    score_scale = 1.0 / math.sqrt(HD)
    queries = seg_queries[0].reshape(tok_rows, KVH, group_size, HD)
    slot_queries = mem_query.reshape(mem_rows, KVH, HD)
    row_pos = tok_index * tok_rows + jnp.arange(tok_rows)

    kv_piece = lax.all_gather(
        jnp.concatenate([seg_keys[0], seg_values[0]], axis=1), "tok", axis=0, tiled=True
    )
    piece_rows = kv_piece.shape[0]
    key_piece = kv_piece[:, :width_kv].reshape(piece_rows, KVH, HD)
    value_piece = kv_piece[:, width_kv:].reshape(piece_rows, KVH, HD)

    live_keys = jnp.arange(piece_rows) < length
    slot_scores = (
        jnp.einsum("rgd,ugd->gru", slot_queries, key_piece, preferred_element_type=jnp.float32)
        * score_scale
    )
    slot_scores = jnp.where(live_keys, slot_scores, neg_fill)
    slot_top = jnp.max(slot_scores, axis=-1, keepdims=True)
    slot_exp = jnp.where(live_keys, jnp.exp(slot_scores - slot_top), 0.0)
    slot_denom = jnp.transpose(jnp.sum(slot_exp, axis=-1))[..., None]
    slot_weights = slot_exp.astype(jnp.bfloat16)
    slot_keys = jnp.einsum(
        "gru,ugd->rgd", slot_weights, key_piece, preferred_element_type=jnp.float32
    )
    slot_values = jnp.einsum(
        "gru,ugd->rgd", slot_weights, value_piece, preferred_element_type=jnp.float32
    )
    raw_slots = jnp.concatenate(
        [
            (slot_keys / slot_denom).reshape(mem_rows, width_kv),
            (slot_values / slot_denom).reshape(mem_rows, width_kv),
        ],
        axis=1,
    )
    written = slot_norm(raw_slots)
    ret_row = retention[0]
    following = doc_start[jnp.minimum(seg_index + 1, seg_count - 1)].astype(jnp.float32)
    keep_flag = jnp.where(seg_index == seg_count - 1, 1.0, 1.0 - following)
    decay_rate = keep_flag * ret_row
    carried = keep_flag * (1.0 - ret_row) * written + (1.0 - keep_flag) * mem_init

    chain_terms = gathered(
        jnp.concatenate([carried, decay_rate[None]], axis=0), "seg", ((2, 3), (0, 1))
    )
    all_carried = chain_terms[:, :mem_rows]
    all_decay = chain_terms[:, mem_rows]
    memory_in = mem_init
    for step in range(seg_count - 1):
        following_memory = all_decay[step] * memory_in + all_carried[step]
        memory_in = jnp.where(step < seg_index, following_memory, memory_in)

    block_rows = math.gcd(piece_rows, 1024)
    blocks = piece_rows // block_rows
    running = (
        jnp.full((KVH, group_size, tok_rows), neg_fill, jnp.float32),
        jnp.zeros((KVH, group_size, tok_rows), jnp.float32),
        jnp.zeros((tok_rows, KVH, group_size, HD), jnp.float32),
    )
    for block in range(blocks):
        block_start = block * block_rows
        key_block = key_piece[block_start : block_start + block_rows]
        value_block = value_piece[block_start : block_start + block_rows]
        columns = block_start + jnp.arange(block_rows)
        causal = (columns[None, :] <= row_pos[:, None]) & (columns < length)[None, :]
        seg_scores = (
            jnp.einsum("tgjd,ugd->gjtu", queries, key_block, preferred_element_type=jnp.float32)
            * score_scale
        )
        seg_top, seg_total, seg_weights, seg_factor = softmax_step(
            running[0], running[1], seg_scores, causal
        )
        seg_acc = running[2] * jnp.transpose(seg_factor, (2, 0, 1))[..., None] + jnp.einsum(
            "gjtu,ugd->tgjd", seg_weights, value_block, preferred_element_type=jnp.float32
        )
        running = (seg_top, seg_total, seg_acc)

    memory_all = gathered(memory_in.astype(jnp.bfloat16), "tok", ((4,), (3,), (2,), (1,), (0,))).reshape(
        -1, 2 * width_kv
    )
    mem_keys = memory_all[:, :width_kv].reshape(-1, KVH, HD)
    mem_vals = memory_all[:, width_kv:].reshape(-1, KVH, HD)
    mem_scores = (
        jnp.einsum("tgjd,mgd->gjtm", queries, mem_keys, preferred_element_type=jnp.float32)
        * score_scale
    )
    row_top = jnp.maximum(running[0], jnp.max(mem_scores, axis=-1))
    seg_factor = jnp.exp(running[0] - row_top)
    mem_weights = jnp.exp(mem_scores - row_top[..., None])
    row_total = running[1] * seg_factor + jnp.sum(mem_weights, axis=-1)
    weighted = running[2] * jnp.transpose(seg_factor, (2, 0, 1))[..., None] + jnp.einsum(
        "gjtm,mgd->tgjd",
        mem_weights.astype(jnp.bfloat16),
        mem_vals,
        preferred_element_type=jnp.float32,
    )
    att_rows = weighted / jnp.transpose(row_total, (2, 0, 1))[..., None]
    log_total = row_top + jnp.log(row_total)
    attended = att_rows.reshape(1, tok_rows, QH * HD).astype(jnp.bfloat16)
    valid_rows = (row_pos < length).astype(jnp.bfloat16)[:, None]
    cotangent = (grad_out[0] * valid_rows * loss_scale).reshape(tok_rows, KVH, group_size, HD)
    row_delta = jnp.einsum("tgjd,tgjd->gjt", cotangent.astype(jnp.float32), att_rows)
    mem_prob = jnp.exp(mem_scores - log_total[..., None])
    grad_prob = jnp.einsum(
        "tgjd,mgd->gjtm", cotangent, mem_vals, preferred_element_type=jnp.float32
    )
    grad_score = mem_prob * (grad_prob - row_delta[..., None])
    grad_vals = jnp.einsum(
        "gjtm,tgjd->mgd",
        mem_prob.astype(jnp.bfloat16),
        cotangent,
        preferred_element_type=jnp.float32,
    )
    grad_keys = (
        jnp.einsum(
            "gjtm,tgjd->mgd",
            grad_score.astype(jnp.bfloat16),
            queries,
            preferred_element_type=jnp.float32,
        )
        * score_scale
    )
    grad_slots = jnp.concatenate(
        [grad_keys.reshape(-1, width_kv), grad_vals.reshape(-1, width_kv)], axis=1
    )
    local_grad = scattered_sum(grad_slots, "tok", (1, 2, 2))

    all_local = gathered(local_grad, "seg", ((2, 3), (0, 1)))
    memory_grad = all_local[seg_count - 1]
    for step in range(seg_count - 2, -1, -1):
        earlier_grad = all_local[step] + all_decay[step] * memory_grad
        memory_grad = jnp.where(step >= seg_index, earlier_grad, memory_grad)
    return (attended, memory_in[None], memory_grad[None])


def solution(mesh):
    placed = (
        P("seg", "tok", None),
        P("seg", "tok", None),
        P("seg", "tok", None),
        P("seg", "tok", None),
        P("tok", None),
        P("tok", None),
        P("seg", None),
        P(),
        P(),
    )
    return jax.shard_map(
        shards,
        mesh=mesh,
        in_specs=placed,
        out_specs=(P("seg", "tok", None), P("seg", "tok", None), P("seg", "tok", None)),
        check_vma=False,
    )
```
